512 devices in a mesh: ta: 32 (over y, x), pb: 16 (over z, core).
Axes of the slice: x: 4, y: 8, z: 8, core: 2. Of those that a mesh axis runs over, the one named last changes fastest.
Arguments:
- particles: float32 [2, 2097152], P(None, ('ta', 'pb')), may hold values from -6 to 6
- weights: bfloat16 [2097152], P(('ta', 'pb')), may hold values from 0.5 to 2
- cell_index: int32 [2097152], P(('ta', 'pb')), may hold values from 0 to 9215
- target_group: int32 [2097152, 1], P(('ta', 'pb')), may hold values from 0 to 31; in each aligned block of 4096 rows (0 to 4095, 4096 to 8191, ...) at most 256 rows name the same one
- target_slice: int32 [2097152], P(('ta', 'pb')), may hold values from 0 to 3
- laser_x: float32 [96], replicated, may hold values from 0.3 to 1.5
- laser_y: float32 [96], replicated, may hold values from 0.3 to 1.5
- mode_x: float32 [96], replicated, may hold values from 0.3 to 1.5
- mode_y: float32 [96], replicated, may hold values from 0.3 to 1.5
- along_coeff: float32 [96, 96], replicated, may hold values from 0.2 to 2
- across_coeff: float32 [96, 96], replicated, may hold values from 0.1 to 1
Outputs:
- arrivals: float32 [2, 4194304], P(None, ('ta', 'pb'))
- radiation: float32 [2, 128], P(None, 'ta')
The draws below stay inside these ranges and needn't reach their ends.
Inputs may be any that keep to these rules, and one draw needn't show every extreme that they name: `target_group`: in the rows of one device at most 256 rows name the same group, and in every draw some group is named by exactly 256 rows of some device.
All inputs are finite; a program needn't handle non-finite values.
Results may differ from the reference program's by a relative error of at most 0.0009.
Values sent between devices are 32-bit elements; how exact they have to be, the bound alone decides.
No kernel may reach another device: no remote copies, remote signals or barrier semaphores. Data moves between devices by JAX's collectives and lax.ppermute only.
A program may use at most 64 MiB of HBM per device.

```python
import math
import jax
import jax.numpy as jnp
import numpy as np
from jax import lax

GX = 96
GY = 96
SL_DEV = 4
PS_DEV = 1024
HARM = 48
PERIODS = 2
PART_DEV = 4096
CAP = 256
SLICES = 128
ROWS = 2097152
N_TA = 32
N_PB = 16


def with_ends(values, stream_key, low, top_value):
    longest = values.shape.index(max(values.shape))
    spots = []
    for shift in (0, 1):
        where = [jax.random.randint(jax.random.fold_in(stream_key, axis), (), 0, length) for axis, length in enumerate(values.shape)]
        where[longest] = (where[longest] + shift) % values.shape[longest]
        spots.append(tuple(where))
    return values.at[spots[0]].set(low).at[spots[1]].set(top_value)


def block_scale(own_key, extent, cuts, smallest, top_value):
    gain = 1.0
    for axis_at, parts in cuts:
        steps = jax.random.uniform(jax.random.fold_in(jax.random.fold_in(own_key, 6), axis_at), (parts,), jnp.float32, smallest / len(cuts), top_value / len(cuts))
        gain = gain * jnp.repeat(jnp.exp(steps), extent[axis_at] // parts).reshape((-1,) + (1,) * (len(extent) - 1 - axis_at))
    return gain


def deal_out(rng, own, number, rows, number_of, top, reach, slope):
    sequence = jax.random.permutation(rng, number_of)
    heavy_load, common = shares(number_of, rows * top, reach, slope, True), shares(number_of, rows * top, reach, slope, False)
    places = jnp.arange(number_of)

    def named(tallies, rotation):
        used = int((tallies > 0).sum())
        fixed = max(1, used // 4)
        passed = fixed + (places - fixed + rotation * (used - fixed)) % max(1, number_of - fixed)
        return jnp.zeros((number_of,), jnp.int32).at[sequence[jnp.where(places < fixed, places, passed)]].set(jnp.asarray(tallies, jnp.int32))

    tallies = jnp.where(number % 4 == 0, named(heavy_load, number // 4), named(common, number - number // 4 - 1))
    mixed = jax.random.permutation(jax.random.fold_in(own, 3), number_of)
    giver, sink = mixed[0:number_of // 2 * 2:2], mixed[1:number_of // 2 * 2:2]
    margin = jnp.minimum(tallies[giver] - 1, reach - tallies[sink]) // 2
    margin = jnp.where((giver == sequence[0]) | (sink == sequence[0]) | (tallies[sink] == 0), 0, jnp.maximum(margin, 0))
    passed = jax.random.randint(jax.random.fold_in(own, 4), (number_of // 2,), 0, 1 << 20) % (margin + 1)
    tallies = tallies.at[giver].add(-passed).at[sink].add(passed)
    members = jnp.searchsorted(jnp.cumsum(tallies), jnp.arange(rows * top), side="right").astype(jnp.int32)
    table = members.reshape(top, rows).T
    table = table[jax.random.permutation(jax.random.fold_in(own, 1), rows)]
    rotation = jax.random.randint(jax.random.fold_in(own, 2), (rows, 1), 0, top)
    return jnp.take_along_axis(table, (jnp.arange(top)[None, :] + rotation) % top, axis=1)


def shares(count, total, limit, slope, full):
    loads = [(1 << 20) // math.isqrt(grade ** slope) + 1 for grade in range(1, count + 1)]
    largest = limit if full else min(limit, max(-(-total // count), total * loads[0] // sum(loads)))
    least = 1 if total - largest >= count - 1 else 0
    given, spare = [largest] + [least] * (count - 1), total - largest - least * (count - 1)
    while spare > 0:
        movable = [i for i in range(1, count) if given[i] < largest] or [i for i in range(1, count) if given[i] < limit]
        mass, left = sum([loads[i] for i in movable]), spare
        for i in movable:
            more = min(limit - given[i], max(1, left * loads[i] // mass), spare)
            given[i] = given[i] + more
            spare = spare - more
    return np.array(given)


def normal_values(rng, dims, width, bound, cuts=(), held_as=jnp.bfloat16):
    loudness = block_scale(rng, dims, cuts, -0.22, 0.18) if cuts else 1.0
    values = jax.random.normal(rng, dims, jnp.float32) * width * loudness
    return jnp.minimum(jnp.maximum(values, -bound), bound).astype(held_as)


def setup_inputs(seed: int = 0) -> dict:
    keys = jax.random.split(jax.random.key(seed), 12)
    particles = normal_values(keys[0], (2, ROWS), 1.0, 6.0, ((1, 512),), jnp.float32)
    weights = jnp.clip(jnp.exp(math.log(2.0) - 1.3862944 * jax.random.uniform(keys[1], (ROWS,), jnp.float32) ** block_scale(keys[1], (ROWS,), ((0, 512),), -0.2, 0.2)), 0.5, 2.0).astype(jnp.bfloat16)
    cell_index = with_ends(jax.random.randint(keys[2], (ROWS,), 0, GX * GY), jax.random.fold_in(keys[2], 1), 0, (GX * GY) - 1).astype(jnp.int32)
    target_group_keys = jax.random.split(jax.random.fold_in(keys[3], 1), ROWS // PART_DEV)
    target_group_turns = jax.random.permutation(jax.random.fold_in(keys[3], 3), ROWS // PART_DEV)
    target_group = jax.vmap(lambda own, number: deal_out(jax.random.fold_in(keys[3], 2), own, number, PART_DEV, N_TA, 1, CAP, 2))(target_group_keys, target_group_turns).reshape((ROWS, 1))
    target_slice = with_ends(jax.random.randint(keys[4], (ROWS,), 0, SL_DEV), jax.random.fold_in(keys[4], 1), 0, SL_DEV - 1).astype(jnp.int32)
    laser_x = jnp.clip(jnp.exp(jax.random.uniform(keys[5], (GX,), jnp.float32, math.log(0.3), math.log(1.5))), 0.3, 1.5)
    laser_y = jnp.clip(jnp.exp(jax.random.uniform(keys[6], (GY,), jnp.float32, math.log(0.3), math.log(1.5))), 0.3, 1.5)
    mode_x = jnp.clip(jnp.exp(jax.random.uniform(keys[7], (GX,), jnp.float32, math.log(0.3), math.log(1.5))), 0.3, 1.5)
    mode_y = jnp.clip(jnp.exp(jax.random.uniform(keys[8], (GY,), jnp.float32, math.log(0.3), math.log(1.5))), 0.3, 1.5)
    along_coeff = jnp.clip(jnp.exp(jax.random.uniform(keys[9], (GX, GY), jnp.float32, math.log(0.2), math.log(2.0))), 0.2, 2.0)
    across_coeff = jnp.clip(jnp.exp(jax.random.uniform(keys[10], (GX, GY), jnp.float32, math.log(0.1), math.log(1.0))), 0.1, 1.0)
    return dict(particles=particles, weights=weights, cell_index=cell_index, target_group=target_group, target_slice=target_slice, laser_x=laser_x, laser_y=laser_y, mode_x=mode_x, mode_y=mode_y, along_coeff=along_coeff, across_coeff=across_coeff)


DISPERSION = 3.0
LASER_GAIN = 1.0
KICK_GAIN = 0.5
SLIP_GAIN = 0.05

def arrival_slots(destination):
    onehot = (destination[:, None] == jnp.arange(N_TA, dtype=jnp.int32)[None, :]).astype(jnp.int32)
    earlier = jnp.cumsum(onehot, axis=0) - onehot
    return lax.optimization_barrier(jnp.sum(earlier * onehot, axis=1)).astype(jnp.int32)

def reference(particles, weights, cell_index, target_group, target_slice, laser_x, laser_y, mode_x, mode_y, along_coeff, across_coeff):
    row_x = cell_index // GY
    row_y = cell_index % GY
    energy = particles[1] + LASER_GAIN * laser_x[row_x] * laser_y[row_y] * jnp.sin(particles[0])
    phases = particles[0] + DISPERSION * energy
    destination = target_group[:, 0]
    devices = N_TA * N_PB
    arrival = lax.map(arrival_slots, destination.reshape(devices, PART_DEV)).reshape(ROWS)
    source = jnp.arange(ROWS, dtype=jnp.int32) // PART_DEV
    target = ((destination * N_PB + source % N_PB) * N_TA + source // N_PB) * CAP + arrival
    total_slots = devices * N_TA * CAP
    got_phase = jnp.zeros(total_slots, jnp.float32).at[target].set(phases)
    got_energy = jnp.zeros(total_slots, jnp.float32).at[target].set(energy)
    got_weight = jnp.zeros(total_slots, jnp.float32).at[target].set(weights.astype(jnp.float32))
    occupied = jnp.zeros(total_slots, jnp.float32).at[target].set(1.0)
    got_slice = jnp.zeros(total_slots, jnp.int32).at[target].set(destination * SL_DEV + target_slice)
    got_cell = jnp.zeros(total_slots, jnp.int32).at[target].set(cell_index)
    cell_count = GX * GY
    density = jax.ops.segment_sum(got_weight, got_slice * cell_count + got_cell, num_segments=SLICES * cell_count)
    density = density.reshape(SLICES, GX, GY)
    padded = jnp.pad(density, 1)
    along_diff = padded[2:, 1:-1, 1:-1] - padded[:-2, 1:-1, 1:-1]
    sideways = padded[1:-1, 2:, 1:-1] + padded[1:-1, :-2, 1:-1] + padded[1:-1, 1:-1, 2:] + padded[1:-1, 1:-1, :-2]
    force_map = along_coeff[None] * along_diff + across_coeff[None] * (4.0 * density - sideways)
    kicked = got_energy + force_map.reshape(-1)[got_slice * cell_count + got_cell]
    profile = mode_x[got_cell // GY] * mode_y[got_cell % GY]
    couple = 1.0 / jnp.sqrt(jnp.float32(N_PB * PS_DEV))
    weighted = got_weight * profile
    radiation = jnp.zeros((2, SLICES), jnp.float32)
    for period in range(PERIODS):
        harmonic_phase = HARM * got_phase
        cosine = jnp.cos(harmonic_phase)
        sine_part = jnp.sin(harmonic_phase)
        real_sum = jax.ops.segment_sum(weighted * cosine, got_slice, num_segments=SLICES)
        imag_sum = jax.ops.segment_sum(-weighted * sine_part, got_slice, num_segments=SLICES)
        radiation = radiation + couple * jnp.stack([real_sum, imag_sum])
        real_here = radiation[0][got_slice]
        imag_here = radiation[1][got_slice]
        kicked = kicked + KICK_GAIN * profile * (real_here * cosine - imag_here * sine_part)
        got_phase = got_phase + SLIP_GAIN * kicked
        radiation = jnp.concatenate([jnp.zeros((2, 1), jnp.float32), radiation[:, :-1]], axis=1)
    filled = occupied > 0.0
    result = jnp.stack([jnp.where(filled, got_phase, 0.0), jnp.where(filled, kicked, 0.0)])
    return (result, radiation)
```

```python
import math

import jax
import jax.numpy as jnp
from jax import lax
from jax.sharding import PartitionSpec as P

SL_DEV = 4
PS_DEV = 1024
HARM = 48
PERIODS = 2


DISPERSION = 3.0
LASER_GAIN = 1.0
KICK_GAIN = 0.5
SLIP_GAIN = 0.05


def shifted(value, axis, steps):
    count = lax.axis_size(axis)
    leading, last = (max(0, -steps), min(count, count - steps))
    return lax.ppermute(value, axis, [(source, source + steps) for source in range(leading, last)])


def lookup(values_table, positions):
    matches = positions[None, :] == jnp.arange(values_table.shape[0], dtype=jnp.int32)[:, None]
    return jnp.sum(jnp.where(matches, values_table[:, None], 0.0), axis=0)


def split3(x):
    hi = lax.reduce_precision(x, exponent_bits=8, mantissa_bits=7)
    rest = x - hi
    mid = lax.reduce_precision(rest, exponent_bits=8, mantissa_bits=7)
    lo = rest - mid
    return [part.astype(jnp.bfloat16) for part in (hi, mid, lo)]


def arrival_slots(destination, groups):
    count = destination.shape[0]
    block_size = math.gcd(count, 512)
    turn_count = count // block_size
    onehot = (destination[:, None] == jnp.arange(groups, dtype=jnp.int32)[None, :]).astype(
        jnp.bfloat16
    )
    onehot = onehot.reshape(turn_count, block_size, groups)
    earlier = (jnp.arange(block_size)[:, None] > jnp.arange(block_size)[None, :]).astype(
        jnp.bfloat16
    )

    def count_step(counted, onehot_rows):
        before = (
            jnp.dot(earlier, onehot_rows, preferred_element_type=jnp.float32) + counted[None, :]
        )
        rows_f = onehot_rows.astype(jnp.float32)
        return (counted + jnp.sum(rows_f, axis=0), jnp.sum(before * rows_f, axis=1))

    _, arrival = lax.scan(count_step, jnp.zeros((groups,), jnp.float32), onehot)
    return arrival.reshape(count).astype(jnp.int32)


def deposit_rows(weight_bf16, row_key, col, targets, grid_y):
    left = jnp.where(
        row_key[None, :] == targets[:, None], weight_bf16[None, :], jnp.zeros((), jnp.bfloat16)
    )
    right = (col[:, None] == jnp.arange(grid_y, dtype=jnp.int32)[None, :]).astype(jnp.bfloat16)
    return jnp.dot(left, right, preferred_element_type=jnp.float32)


def pb_sum(flat, axis):
    count = lax.axis_size(axis)
    chunks = flat.reshape(count, -1)
    mine = jnp.sum(lax.all_to_all(chunks, axis, 0, 0, tiled=True), axis=0)
    every = lax.all_to_all(jnp.broadcast_to(mine[None], chunks.shape), axis, 0, 0, tiled=True)
    return every.reshape(-1)


def pb_sum_small(value, axis):
    count = lax.axis_size(axis)
    spread = jnp.broadcast_to(value[None], (count,) + value.shape)
    return jnp.sum(lax.all_to_all(spread, axis, 0, 0, tiled=True), axis=0)


def stencil(extended, sideways, coeff_long, coeff_cross, grid_y):
    centre = sideways[:, grid_y:-grid_y]
    along_diff = extended[2:] - extended[:-2]
    across = sideways[:, 2 * grid_y :] + sideways[:, : -2 * grid_y]
    column = jnp.arange(centre.shape[1], dtype=jnp.int32) % grid_y
    upper_y = jnp.where(column < grid_y - 1, jnp.pad(centre, ((0, 0), (0, 1)))[:, 1:], 0.0)
    lower_y = jnp.where(column > 0, jnp.pad(centre, ((0, 0), (1, 0)))[:, :-1], 0.0)
    return coeff_long[None, :] * along_diff + coeff_cross[None, :] * (
        4.0 * centre - across - upper_y - lower_y
    )


def body(
    particles,
    weights,
    cell_index,
    target_group,
    target_slice,
    laser_x,
    laser_y,
    mode_x,
    mode_y,
    along_coeff,
    across_coeff,
):
    groups = lax.axis_size("ta")
    splits = lax.axis_size("pb")
    grid_x = laser_x.shape[0]
    grid_y = laser_y.shape[0]
    cell_count = grid_x * grid_y
    per_device = particles.shape[1]
    capacity = 2 * per_device // groups
    slot_count = groups * capacity
    row_x = cell_index // grid_y
    row_y = cell_index % grid_y
    energy = particles[1] + LASER_GAIN * lookup(laser_x, row_x) * lookup(laser_y, row_y) * jnp.sin(
        particles[0]
    )
    phases = particles[0] + DISPERSION * energy
    destination = target_group[:, 0]
    arrival = arrival_slots(destination, groups)

    values = jnp.stack(
        [
            phases,
            energy,
            weights.astype(jnp.float32),
            (target_slice * cell_count + cell_index).astype(jnp.float32),
        ]
    )
    value_count = values.shape[0]
    to_group = destination[None, :] == jnp.arange(groups, dtype=jnp.int32)[:, None]
    parts = split3(values)
    left = jnp.concatenate(
        [
            jnp.where(to_group[None], part[:, None, :], jnp.zeros((), jnp.bfloat16)).reshape(
                value_count * groups, per_device
            )
            for part in parts
        ]
    )
    to_slot = (arrival[:, None] == jnp.arange(capacity, dtype=jnp.int32)[None, :]).astype(
        jnp.bfloat16
    )
    placed = jnp.dot(left, to_slot, preferred_element_type=jnp.float32)
    rows = value_count * groups
    send = (placed[:rows] + placed[rows : 2 * rows]) + placed[2 * rows :]
    got = lax.all_to_all(
        send.reshape(value_count, groups, capacity), "ta", split_axis=1, concat_axis=1, tiled=True
    ).reshape(value_count, slot_count)

    got_phase = got[0]
    got_energy = got[1]
    arrived_weight = got[2]
    combined = got[3].astype(jnp.int32)
    got_slice = combined // cell_count
    got_cell = combined % cell_count
    got_x = got_cell // grid_y
    got_y = got_cell % grid_y
    row_key = got_slice * grid_x + got_x
    weight_bf16 = arrived_weight.astype(jnp.bfloat16)

    edge_targets = jnp.concatenate(
        [
            jnp.arange(grid_x, dtype=jnp.int32),
            jnp.arange(grid_x, dtype=jnp.int32) + (SL_DEV - 1) * grid_x,
        ]
    )
    edges = deposit_rows(weight_bf16, row_key, got_y, edge_targets, grid_y).reshape(2, cell_count)
    below = shifted(edges[1:2], "ta", 1)
    above = shifted(edges[0:1], "ta", -1)
    middle_targets = jnp.arange(grid_x, (SL_DEV - 1) * grid_x, dtype=jnp.int32)
    middle = deposit_rows(weight_bf16, row_key, got_y, middle_targets, grid_y).reshape(
        SL_DEV - 2, cell_count
    )

    profile = lookup(mode_x, got_x) * lookup(mode_y, got_y)
    weighted = arrived_weight * profile
    select = (got_slice[None, :] == jnp.arange(SL_DEV, dtype=jnp.int32)[:, None]).astype(
        jnp.float32
    )

    def local_bunching(phase):
        harmonic_phase = HARM * phase
        cosine = jnp.cos(harmonic_phase)
        sine_part = jnp.sin(harmonic_phase)
        sums = jnp.stack(
            [
                jnp.sum(select * (weighted * cosine)[None, :], axis=1),
                jnp.sum(select * (-weighted * sine_part)[None, :], axis=1),
            ]
        )
        return cosine, sine_part, sums

    cosine0, sine0, sums0 = local_bunching(got_phase)
    stacked = jnp.concatenate(
        [below.reshape(-1), edges[0], middle.reshape(-1), edges[1], above.reshape(-1), sums0.reshape(-1)]
    )
    width = splits * 8
    padded_len = -(-stacked.shape[0] // width) * width
    stacked = jnp.pad(stacked, (0, padded_len - stacked.shape[0]))
    summed = pb_sum(stacked, "pb")
    extended = summed[: (SL_DEV + 2) * cell_count].reshape(SL_DEV + 2, cell_count)
    bunching0 = summed[(SL_DEV + 2) * cell_count : (SL_DEV + 2) * cell_count + 2 * SL_DEV].reshape(
        2, SL_DEV
    )

    long_flat = along_coeff.reshape(cell_count)
    cross_flat = across_coeff.reshape(cell_count)
    sideways = jnp.pad(extended[1:-1], ((0, 0), (grid_y, grid_y)))
    force_map = stencil(extended, sideways, long_flat, cross_flat, grid_y)

    force_rows = force_map.reshape(SL_DEV * grid_x, grid_y)
    force_parts = jnp.concatenate(split3(force_rows), axis=1)
    pick_row = (row_key[:, None] == jnp.arange(SL_DEV * grid_x, dtype=jnp.int32)[None, :]).astype(
        jnp.bfloat16
    )
    picked = jnp.dot(pick_row, force_parts, preferred_element_type=jnp.float32)
    picked = (picked[:, :grid_y] + picked[:, grid_y : 2 * grid_y]) + picked[:, 2 * grid_y :]
    pick_col = got_y[:, None] == jnp.arange(grid_y, dtype=jnp.int32)[None, :]
    kicked = got_energy + jnp.sum(jnp.where(pick_col, picked, 0.0), axis=1)

    couple = 1.0 / math.sqrt(splits * PS_DEV)
    radiation = jnp.zeros((2, SL_DEV), jnp.float32)
    for period in range(PERIODS):
        if period == 0:
            cosine, sine_part, bunching = cosine0, sine0, bunching0
        else:
            cosine, sine_part, local_sums = local_bunching(got_phase)
            bunching = pb_sum_small(local_sums, "pb")
        radiation = radiation + couple * bunching
        real_here = jnp.sum(select * radiation[0][:, None], axis=0)
        imag_here = jnp.sum(select * radiation[1][:, None], axis=0)
        kicked = kicked + KICK_GAIN * profile * (real_here * cosine - imag_here * sine_part)
        got_phase = got_phase + SLIP_GAIN * kicked
        incoming = shifted(radiation[:, -1:], "ta", 1)
        radiation = jnp.concatenate([incoming, radiation[:, :-1]], axis=1)
    filled = arrived_weight > 0
    result = jnp.stack([jnp.where(filled, got_phase, 0.0), jnp.where(filled, kicked, 0.0)])
    return (result, radiation)


def solution(mesh):
    return jax.shard_map(
        body,
        mesh=mesh,
        in_specs=(
            P(None, ("ta", "pb")),
            P(("ta", "pb")),
            P(("ta", "pb")),
            P(("ta", "pb"), None),
            P(("ta", "pb")),
            P(),
            P(),
            P(),
            P(),
            P(),
            P(),
        ),
        out_specs=(P(None, ("ta", "pb")), P(None, "ta")),
        check_vma=False,
    )
```

```python
import math

import jax
import jax.numpy as jnp
from jax import lax
from jax.sharding import PartitionSpec as P

SL_DEV = 4
PS_DEV = 1024
HARM = 48
PERIODS = 2


DISPERSION = 3.0
LASER_GAIN = 1.0
KICK_GAIN = 0.5
SLIP_GAIN = 0.05


def shifted(value, axis, steps):
    count = lax.axis_size(axis)
    leading, last = (max(0, -steps), min(count, count - steps))
    return lax.ppermute(value, axis, [(source, source + steps) for source in range(leading, last)])


def lookup(values_table, positions):
    matches = positions[None, :] == jnp.arange(values_table.shape[0], dtype=jnp.int32)[:, None]
    return jnp.sum(jnp.where(matches, values_table[:, None], 0.0), axis=0)


def split3(x):
    hi = lax.reduce_precision(x, exponent_bits=8, mantissa_bits=7)
    rest = x - hi
    mid = lax.reduce_precision(rest, exponent_bits=8, mantissa_bits=7)
    lo = rest - mid
    return [part.astype(jnp.bfloat16) for part in (hi, mid, lo)]


def arrival_slots(destination, groups):
    count = destination.shape[0]
    block_size = math.gcd(count, 512)
    turn_count = count // block_size
    onehot = (destination[:, None] == jnp.arange(groups, dtype=jnp.int32)[None, :]).astype(
        jnp.bfloat16
    )
    onehot = onehot.reshape(turn_count, block_size, groups)
    earlier = (jnp.arange(block_size)[:, None] > jnp.arange(block_size)[None, :]).astype(
        jnp.bfloat16
    )
    within = jnp.einsum("ij,tjg->tig", earlier, onehot, preferred_element_type=jnp.float32)
    rows_f = onehot.astype(jnp.float32)
    per_turn = jnp.sum(rows_f, axis=1)
    offsets = jnp.cumsum(per_turn, axis=0) - per_turn
    arrival = jnp.sum((within + offsets[:, None, :]) * rows_f, axis=2)
    return arrival.reshape(count).astype(jnp.int32)


def deposit_rows(weight_bf16, row_key, col, targets, grid_y):
    left = jnp.where(
        row_key[None, :] == targets[:, None], weight_bf16[None, :], jnp.zeros((), jnp.bfloat16)
    )
    right = (col[:, None] == jnp.arange(grid_y, dtype=jnp.int32)[None, :]).astype(jnp.bfloat16)
    return jnp.dot(left, right, preferred_element_type=jnp.float32)


def pb_sum(rows, axis):
    count = lax.axis_size(axis)
    chunks = rows.reshape((count, -1) + rows.shape[1:])
    mine = jnp.sum(lax.all_to_all(chunks, axis, 0, 0, tiled=True), axis=0)
    every = lax.all_to_all(jnp.broadcast_to(mine[None], chunks.shape), axis, 0, 0, tiled=True)
    return every.reshape(rows.shape)


def pb_sum_small(value, axis):
    count = lax.axis_size(axis)
    spread = jnp.broadcast_to(value[None], (count,) + value.shape)
    return jnp.sum(lax.all_to_all(spread, axis, 0, 0, tiled=True), axis=0)


def stencil(extended, coeff_long, coeff_cross):
    centre = extended[1:-1]
    along_diff = extended[2:] - extended[:-2]
    padded_x = jnp.pad(centre, ((0, 0), (1, 1), (0, 0)))
    across = padded_x[:, 2:, :] + padded_x[:, :-2, :]
    padded_y = jnp.pad(centre, ((0, 0), (0, 0), (1, 1)))
    upper_y = padded_y[:, :, 2:]
    lower_y = padded_y[:, :, :-2]
    return coeff_long[None] * along_diff + coeff_cross[None] * (
        4.0 * centre - across - upper_y - lower_y
    )


def body(
    particles,
    weights,
    cell_index,
    target_group,
    target_slice,
    laser_x,
    laser_y,
    mode_x,
    mode_y,
    along_coeff,
    across_coeff,
):
    groups = lax.axis_size("ta")
    splits = lax.axis_size("pb")
    grid_x = laser_x.shape[0]
    grid_y = laser_y.shape[0]
    cell_count = grid_x * grid_y
    per_device = particles.shape[1]
    capacity = 2 * per_device // groups
    slot_count = groups * capacity
    row_x = cell_index // grid_y
    row_y = cell_index % grid_y
    energy = particles[1] + LASER_GAIN * lookup(laser_x, row_x) * lookup(laser_y, row_y) * jnp.sin(
        particles[0]
    )
    phases = particles[0] + DISPERSION * energy
    destination = target_group.reshape(-1)
    arrival = arrival_slots(destination, groups)

    values = jnp.stack(
        [
            phases,
            energy,
            weights.astype(jnp.float32),
            (target_slice * cell_count + cell_index).astype(jnp.float32),
        ]
    )
    value_count = values.shape[0]
    to_group = destination[None, :] == jnp.arange(groups, dtype=jnp.int32)[:, None]
    parts = split3(values)
    left = jnp.concatenate(
        [
            jnp.where(to_group[None], part[:, None, :], jnp.zeros((), jnp.bfloat16)).reshape(
                value_count * groups, per_device
            )
            for part in parts
        ]
    )
    to_slot = (arrival[:, None] == jnp.arange(capacity, dtype=jnp.int32)[None, :]).astype(
        jnp.bfloat16
    )
    placed = jnp.dot(left, to_slot, preferred_element_type=jnp.float32)
    rows = value_count * groups
    send = (placed[:rows] + placed[rows : 2 * rows]) + placed[2 * rows :]
    got = lax.all_to_all(
        send.reshape(value_count, groups, capacity), "ta", split_axis=1, concat_axis=1, tiled=True
    ).reshape(value_count, slot_count)

    got_phase = got[0]
    got_energy = got[1]
    arrived_weight = got[2]
    combined = got[3].astype(jnp.int32)
    got_slice = combined // cell_count
    got_cell = combined % cell_count
    got_x = got_cell // grid_y
    got_y = got_cell % grid_y
    row_key = got_slice * grid_x + got_x
    weight_bf16 = arrived_weight.astype(jnp.bfloat16)

    edge_targets = jnp.concatenate(
        [
            jnp.arange(grid_x, dtype=jnp.int32),
            jnp.arange(grid_x, dtype=jnp.int32) + (SL_DEV - 1) * grid_x,
        ]
    )
    edges = deposit_rows(weight_bf16, row_key, got_y, edge_targets, grid_y)
    below = shifted(edges[grid_x:], "ta", 1)
    above = shifted(edges[:grid_x], "ta", -1)
    middle_targets = jnp.arange(grid_x, (SL_DEV - 1) * grid_x, dtype=jnp.int32)
    middle = deposit_rows(weight_bf16, row_key, got_y, middle_targets, grid_y)

    profile = lookup(mode_x, got_x) * lookup(mode_y, got_y)
    weighted = arrived_weight * profile
    select = (got_slice[None, :] == jnp.arange(SL_DEV, dtype=jnp.int32)[:, None]).astype(
        jnp.float32
    )

    def local_bunching(phase):
        harmonic_phase = HARM * phase
        cosine = jnp.cos(harmonic_phase)
        sine_part = jnp.sin(harmonic_phase)
        sums = jnp.stack(
            [
                jnp.sum(select * (weighted * cosine)[None, :], axis=1),
                jnp.sum(select * (-weighted * sine_part)[None, :], axis=1),
            ]
        )
        return cosine, sine_part, sums

    cosine0, sine0, sums0 = local_bunching(got_phase)
    sums_row = jnp.pad(sums0.reshape(1, 2 * SL_DEV), ((0, 7), (0, grid_y - 2 * SL_DEV)))
    stacked = jnp.concatenate([below, edges[:grid_x], middle, edges[grid_x:], above, sums_row])
    chunk_rows = -(-stacked.shape[0] // (splits * 8)) * 8
    stacked = jnp.pad(stacked, ((0, chunk_rows * splits - stacked.shape[0]), (0, 0)))
    summed = pb_sum(stacked, "pb")
    density_rows = (SL_DEV + 2) * grid_x
    extended = summed[:density_rows].reshape(SL_DEV + 2, grid_x, grid_y)
    bunching0 = summed[density_rows, : 2 * SL_DEV].reshape(2, SL_DEV)
    force_map = stencil(extended, along_coeff, across_coeff)

    force_rows = force_map.reshape(SL_DEV * grid_x, grid_y)
    force_hi = lax.reduce_precision(force_rows, exponent_bits=8, mantissa_bits=7)
    force_parts = jnp.concatenate(
        [force_hi.astype(jnp.bfloat16), (force_rows - force_hi).astype(jnp.bfloat16)], axis=1
    )
    pick_row = (row_key[:, None] == jnp.arange(SL_DEV * grid_x, dtype=jnp.int32)[None, :]).astype(
        jnp.bfloat16
    )
    picked = jnp.dot(pick_row, force_parts, preferred_element_type=jnp.float32)
    picked = picked[:, :grid_y] + picked[:, grid_y:]
    pick_col = got_y[:, None] == jnp.arange(grid_y, dtype=jnp.int32)[None, :]
    kicked = got_energy + jnp.sum(jnp.where(pick_col, picked, 0.0), axis=1)

    couple = 1.0 / math.sqrt(splits * PS_DEV)
    radiation = jnp.zeros((2, SL_DEV), jnp.float32)
    for period in range(PERIODS):
        if period == 0:
            cosine, sine_part, bunching = cosine0, sine0, bunching0
        else:
            cosine, sine_part, local_sums = local_bunching(got_phase)
            bunching = pb_sum_small(local_sums, "pb")
        radiation = radiation + couple * bunching
        real_here = jnp.sum(select * radiation[0][:, None], axis=0)
        imag_here = jnp.sum(select * radiation[1][:, None], axis=0)
        kicked = kicked + KICK_GAIN * profile * (real_here * cosine - imag_here * sine_part)
        got_phase = got_phase + SLIP_GAIN * kicked
        incoming = shifted(radiation[:, -1:], "ta", 1)
        radiation = jnp.concatenate([incoming, radiation[:, :-1]], axis=1)
    filled = arrived_weight > 0
    result = jnp.stack([jnp.where(filled, got_phase, 0.0), jnp.where(filled, kicked, 0.0)])
    return (result, radiation)


def solution(mesh):
    return jax.shard_map(
        body,
        mesh=mesh,
        in_specs=(
            P(None, ("ta", "pb")),
            P(("ta", "pb")),
            P(("ta", "pb")),
            P(("ta", "pb"), None),
            P(("ta", "pb")),
            P(),
            P(),
            P(),
            P(),
            P(),
            P(),
        ),
        out_specs=(P(None, ("ta", "pb")), P(None, "ta")),
        check_vma=False,
    )
```

```python
import math

import jax
import jax.numpy as jnp
from jax import lax
from jax.sharding import PartitionSpec as P

SL_DEV = 4
PS_DEV = 1024
HARM = 48
PERIODS = 2


DISPERSION = 3.0
LASER_GAIN = 1.0
KICK_GAIN = 0.5
SLIP_GAIN = 0.05


def shifted(value, axis, steps):
    count = lax.axis_size(axis)
    leading, last = (max(0, -steps), min(count, count - steps))
    return lax.ppermute(value, axis, [(source, source + steps) for source in range(leading, last)])


def lookup(values_table, positions):
    matches = positions[None, :] == jnp.arange(values_table.shape[0], dtype=jnp.int32)[:, None]
    return jnp.sum(jnp.where(matches, values_table[:, None], 0.0), axis=0)


def split3(x):
    hi = lax.reduce_precision(x, exponent_bits=8, mantissa_bits=7)
    rest = x - hi
    mid = lax.reduce_precision(rest, exponent_bits=8, mantissa_bits=7)
    lo = rest - mid
    return [part.astype(jnp.bfloat16) for part in (hi, mid, lo)]


def arrival_slots(to_group):
    groups, count = to_group.shape
    block_size = math.gcd(count, 512)
    turn_count = count // block_size
    onehot = to_group.astype(jnp.bfloat16).reshape(groups, turn_count, block_size)
    earlier = (jnp.arange(block_size)[:, None] > jnp.arange(block_size)[None, :]).astype(
        jnp.bfloat16
    )
    within = jnp.einsum("gtj,ij->gti", onehot, earlier, preferred_element_type=jnp.float32)
    rows_f = onehot.astype(jnp.float32)
    per_turn = jnp.sum(rows_f, axis=2)
    offsets = jnp.cumsum(per_turn, axis=1) - per_turn
    arrival = jnp.sum((within + offsets[:, :, None]) * rows_f, axis=0)
    return arrival.reshape(count).astype(jnp.int32)


def deposit_rows(weight_bf16, row_key, col, targets, grid_y):
    left = jnp.where(
        row_key[None, :] == targets[:, None], weight_bf16[None, :], jnp.zeros((), jnp.bfloat16)
    )
    right = (col[:, None] == jnp.arange(grid_y, dtype=jnp.int32)[None, :]).astype(jnp.bfloat16)
    return jnp.dot(left, right, preferred_element_type=jnp.float32)


def pb_sum(rows, axis):
    count = lax.axis_size(axis)
    chunks = rows.reshape((count, -1) + rows.shape[1:])
    mine = jnp.sum(lax.all_to_all(chunks, axis, 0, 0, tiled=True), axis=0)
    every = lax.all_to_all(jnp.broadcast_to(mine[None], chunks.shape), axis, 0, 0, tiled=True)
    return every.reshape(rows.shape)


def pb_sum_small(value, axis):
    count = lax.axis_size(axis)
    spread = jnp.broadcast_to(value[None], (count,) + value.shape)
    return jnp.sum(lax.all_to_all(spread, axis, 0, 0, tiled=True), axis=0)


def stencil(extended, coeff_long, coeff_cross):
    centre = extended[1:-1]
    along_diff = extended[2:] - extended[:-2]
    padded_x = jnp.pad(centre, ((0, 0), (1, 1), (0, 0)))
    across = padded_x[:, 2:, :] + padded_x[:, :-2, :]
    padded_y = jnp.pad(centre, ((0, 0), (0, 0), (1, 1)))
    upper_y = padded_y[:, :, 2:]
    lower_y = padded_y[:, :, :-2]
    return coeff_long[None] * along_diff + coeff_cross[None] * (
        4.0 * centre - across - upper_y - lower_y
    )


def body(
    particles,
    weights,
    cell_index,
    target_group,
    target_slice,
    laser_x,
    laser_y,
    mode_x,
    mode_y,
    along_coeff,
    across_coeff,
):
    groups = lax.axis_size("ta")
    splits = lax.axis_size("pb")
    grid_x = laser_x.shape[0]
    grid_y = laser_y.shape[0]
    cell_count = grid_x * grid_y
    per_device = particles.shape[1]
    capacity = 2 * per_device // groups
    slot_count = groups * capacity
    row_x = cell_index // grid_y
    row_y = cell_index % grid_y
    energy = particles[1] + LASER_GAIN * lookup(laser_x, row_x) * lookup(laser_y, row_y) * jnp.sin(
        particles[0]
    )
    phases = particles[0] + DISPERSION * energy
    destination = target_group.reshape(1, per_device)
    to_group = destination == jnp.arange(groups, dtype=jnp.int32)[:, None]
    arrival = arrival_slots(to_group)

    values = jnp.stack(
        [
            phases,
            energy,
            weights.astype(jnp.float32),
            (target_slice * cell_count + cell_index).astype(jnp.float32),
        ]
    )
    value_count = values.shape[0]
    parts = split3(values)
    left = jnp.concatenate(
        [
            jnp.where(to_group[None], part[:, None, :], jnp.zeros((), jnp.bfloat16)).reshape(
                value_count * groups, per_device
            )
            for part in parts
        ]
    )
    to_slot = (arrival[:, None] == jnp.arange(capacity, dtype=jnp.int32)[None, :]).astype(
        jnp.bfloat16
    )
    placed = jnp.dot(left, to_slot, preferred_element_type=jnp.float32)
    rows = value_count * groups
    send = (placed[:rows] + placed[rows : 2 * rows]) + placed[2 * rows :]
    got = lax.all_to_all(
        send.reshape(value_count, groups, capacity), "ta", split_axis=1, concat_axis=1, tiled=True
    ).reshape(value_count, slot_count)

    got_phase = got[0]
    got_energy = got[1]
    arrived_weight = got[2]
    combined = got[3].astype(jnp.int32)
    got_slice = combined // cell_count
    got_cell = combined % cell_count
    got_x = got_cell // grid_y
    got_y = got_cell % grid_y
    row_key = got_slice * grid_x + got_x
    weight_bf16 = arrived_weight.astype(jnp.bfloat16)

    edge_targets = jnp.concatenate(
        [
            jnp.arange(grid_x, dtype=jnp.int32),
            jnp.arange(grid_x, dtype=jnp.int32) + (SL_DEV - 1) * grid_x,
        ]
    )
    edges = deposit_rows(weight_bf16, row_key, got_y, edge_targets, grid_y)
    below = shifted(edges[grid_x:], "ta", 1)
    above = shifted(edges[:grid_x], "ta", -1)
    middle_targets = jnp.arange(grid_x, (SL_DEV - 1) * grid_x, dtype=jnp.int32)
    middle = deposit_rows(weight_bf16, row_key, got_y, middle_targets, grid_y)

    profile = lookup(mode_x, got_x) * lookup(mode_y, got_y)
    weighted = arrived_weight * profile
    select = (got_slice[None, :] == jnp.arange(SL_DEV, dtype=jnp.int32)[:, None]).astype(
        jnp.float32
    )

    def local_bunching(phase):
        harmonic_phase = HARM * phase
        cosine = jnp.cos(harmonic_phase)
        sine_part = jnp.sin(harmonic_phase)
        sums = jnp.stack(
            [
                jnp.sum(select * (weighted * cosine)[None, :], axis=1),
                jnp.sum(select * (-weighted * sine_part)[None, :], axis=1),
            ]
        )
        return cosine, sine_part, sums

    cosine0, sine0, sums0 = local_bunching(got_phase)
    sums_row = jnp.pad(sums0.reshape(1, 2 * SL_DEV), ((0, 7), (0, grid_y - 2 * SL_DEV)))
    stacked = jnp.concatenate([below, edges[:grid_x], middle, edges[grid_x:], above, sums_row])
    chunk_rows = -(-stacked.shape[0] // (splits * 8)) * 8
    stacked = jnp.pad(stacked, ((0, chunk_rows * splits - stacked.shape[0]), (0, 0)))
    summed = pb_sum(stacked, "pb")
    density_rows = (SL_DEV + 2) * grid_x
    extended = summed[:density_rows].reshape(SL_DEV + 2, grid_x, grid_y)
    bunching0 = summed[density_rows, : 2 * SL_DEV].reshape(2, SL_DEV)
    force_map = stencil(extended, along_coeff, across_coeff)

    force_rows = force_map.reshape(SL_DEV * grid_x, grid_y)
    force_hi = lax.reduce_precision(force_rows, exponent_bits=8, mantissa_bits=7)
    force_parts = jnp.concatenate(
        [force_hi.astype(jnp.bfloat16), (force_rows - force_hi).astype(jnp.bfloat16)], axis=1
    )
    pick_row = (row_key[:, None] == jnp.arange(SL_DEV * grid_x, dtype=jnp.int32)[None, :]).astype(
        jnp.bfloat16
    )
    picked = jnp.dot(pick_row, force_parts, preferred_element_type=jnp.float32)
    picked = picked[:, :grid_y] + picked[:, grid_y:]
    pick_col = got_y[:, None] == jnp.arange(grid_y, dtype=jnp.int32)[None, :]
    kicked = got_energy + jnp.sum(jnp.where(pick_col, picked, 0.0), axis=1)

    couple = 1.0 / math.sqrt(splits * PS_DEV)
    radiation = jnp.zeros((2, SL_DEV), jnp.float32)
    for period in range(PERIODS):
        if period == 0:
            cosine, sine_part, bunching = cosine0, sine0, bunching0
        else:
            cosine, sine_part, local_sums = local_bunching(got_phase)
            bunching = pb_sum_small(local_sums, "pb")
        radiation = radiation + couple * bunching
        real_here = jnp.sum(select * radiation[0][:, None], axis=0)
        imag_here = jnp.sum(select * radiation[1][:, None], axis=0)
        kicked = kicked + KICK_GAIN * profile * (real_here * cosine - imag_here * sine_part)
        got_phase = got_phase + SLIP_GAIN * kicked
        incoming = shifted(radiation[:, -1:], "ta", 1)
        radiation = jnp.concatenate([incoming, radiation[:, :-1]], axis=1)
    filled = arrived_weight > 0
    result = jnp.stack([jnp.where(filled, got_phase, 0.0), jnp.where(filled, kicked, 0.0)])
    return (result, radiation)


def solution(mesh):
    return jax.shard_map(
        body,
        mesh=mesh,
        in_specs=(
            P(None, ("ta", "pb")),
            P(("ta", "pb")),
            P(("ta", "pb")),
            P(("ta", "pb"), None),
            P(("ta", "pb")),
            P(),
            P(),
            P(),
            P(),
            P(),
            P(),
        ),
        out_specs=(P(None, ("ta", "pb")), P(None, "ta")),
        check_vma=False,
    )
```

```python
import math

import jax
import jax.numpy as jnp
from jax import lax
from jax.sharding import PartitionSpec as P

SL_DEV = 4
PS_DEV = 1024
HARM = 48
PERIODS = 2


DISPERSION = 3.0
LASER_GAIN = 1.0
KICK_GAIN = 0.5
SLIP_GAIN = 0.05


def shifted(value, axis, steps):
    count = lax.axis_size(axis)
    leading, last = (max(0, -steps), min(count, count - steps))
    return lax.ppermute(value, axis, [(source, source + steps) for source in range(leading, last)])


def lookup(values_table, positions):
    matches = positions[None, :] == jnp.arange(values_table.shape[0], dtype=jnp.int32)[:, None]
    return jnp.sum(jnp.where(matches, values_table[:, None], 0.0), axis=0)


def split3(x):
    hi = lax.reduce_precision(x, exponent_bits=8, mantissa_bits=7)
    rest = x - hi
    mid = lax.reduce_precision(rest, exponent_bits=8, mantissa_bits=7)
    lo = rest - mid
    return [part.astype(jnp.bfloat16) for part in (hi, mid, lo)]


def arrival_slots(to_group):
    groups, count = to_group.shape
    block_size = math.gcd(count, 512)
    turn_count = count // block_size
    onehot = to_group.astype(jnp.bfloat16).reshape(groups, turn_count, block_size)
    earlier = (jnp.arange(block_size)[:, None] > jnp.arange(block_size)[None, :]).astype(
        jnp.bfloat16
    )
    within = jnp.einsum("gtj,ij->gti", onehot, earlier, preferred_element_type=jnp.float32)
    rows_f = onehot.astype(jnp.float32)
    per_turn = jnp.sum(rows_f, axis=2)
    offsets = jnp.cumsum(per_turn, axis=1) - per_turn
    arrival = jnp.sum((within + offsets[:, :, None]) * rows_f, axis=0)
    return arrival.reshape(count).astype(jnp.int32)


def deposit_rows(weight_bf16, row_key, col, targets, grid_y):
    left = jnp.where(
        row_key[None, :] == targets[:, None], weight_bf16[None, :], jnp.zeros((), jnp.bfloat16)
    )
    right = (col[:, None] == jnp.arange(grid_y, dtype=jnp.int32)[None, :]).astype(jnp.bfloat16)
    return jnp.dot(left, right, preferred_element_type=jnp.float32)


def pb_sum(rows, axis):
    count = lax.axis_size(axis)
    chunks = rows.reshape((count, -1) + rows.shape[1:])
    mine = jnp.sum(lax.all_to_all(chunks, axis, 0, 0, tiled=True), axis=0)
    every = lax.all_to_all(jnp.broadcast_to(mine[None], chunks.shape), axis, 0, 0, tiled=True)
    return every.reshape(rows.shape)


def pb_sum_small(value, axis):
    count = lax.axis_size(axis)
    spread = jnp.broadcast_to(value[None], (count,) + value.shape)
    return jnp.sum(lax.all_to_all(spread, axis, 0, 0, tiled=True), axis=0)


def stencil(extended, coeff_long, coeff_cross):
    centre = extended[1:-1]
    along_diff = extended[2:] - extended[:-2]
    padded_x = jnp.pad(centre, ((0, 0), (1, 1), (0, 0)))
    across = padded_x[:, 2:, :] + padded_x[:, :-2, :]
    padded_y = jnp.pad(centre, ((0, 0), (0, 0), (1, 1)))
    upper_y = padded_y[:, :, 2:]
    lower_y = padded_y[:, :, :-2]
    return coeff_long[None] * along_diff + coeff_cross[None] * (
        4.0 * centre - across - upper_y - lower_y
    )


def body(
    particles,
    weights,
    cell_index,
    target_group,
    target_slice,
    laser_x,
    laser_y,
    mode_x,
    mode_y,
    along_coeff,
    across_coeff,
):
    groups = lax.axis_size("ta")
    splits = lax.axis_size("pb")
    grid_x = laser_x.shape[0]
    grid_y = laser_y.shape[0]
    cell_count = grid_x * grid_y
    per_device = particles.shape[1]
    capacity = 2 * per_device // groups
    slot_count = groups * capacity
    row_x = cell_index // grid_y
    row_y = cell_index % grid_y
    energy = particles[1] + LASER_GAIN * lookup(laser_x, row_x) * lookup(laser_y, row_y) * jnp.sin(
        particles[0]
    )
    phases = particles[0] + DISPERSION * energy
    destination = target_group.reshape(1, per_device)
    to_group = destination == jnp.arange(groups, dtype=jnp.int32)[:, None]
    arrival = arrival_slots(to_group)

    values = jnp.stack(
        [
            phases,
            energy,
            weights.astype(jnp.float32),
            (target_slice * cell_count + cell_index).astype(jnp.float32),
        ]
    )
    value_count = values.shape[0]
    parts = split3(values)
    left = jnp.concatenate(
        [
            jnp.where(to_group[None], part[:, None, :], jnp.zeros((), jnp.bfloat16)).reshape(
                value_count * groups, per_device
            )
            for part in parts
        ]
    )
    to_slot = (arrival[:, None] == jnp.arange(capacity, dtype=jnp.int32)[None, :]).astype(
        jnp.bfloat16
    )
    placed = jnp.dot(left, to_slot, preferred_element_type=jnp.float32)
    rows = value_count * groups
    send = (placed[:rows] + placed[rows : 2 * rows]) + placed[2 * rows :]
    got = lax.all_to_all(
        send.reshape(value_count, groups, capacity), "ta", split_axis=1, concat_axis=1, tiled=True
    ).reshape(value_count, slot_count)

    got_phase = got[0]
    got_energy = got[1]
    arrived_weight = got[2]
    combined = got[3].astype(jnp.int32)
    got_slice = combined // cell_count
    got_cell = combined % cell_count
    got_x = got_cell // grid_y
    got_y = got_cell % grid_y
    row_key = got_slice * grid_x + got_x
    weight_bf16 = arrived_weight.astype(jnp.bfloat16)

    density_rows = SL_DEV * grid_x
    partial = deposit_rows(
        weight_bf16, row_key, got_y, jnp.arange(density_rows, dtype=jnp.int32), grid_y
    )

    profile = lookup(mode_x, got_x) * lookup(mode_y, got_y)
    weighted = arrived_weight * profile
    select = (got_slice[None, :] == jnp.arange(SL_DEV, dtype=jnp.int32)[:, None]).astype(
        jnp.float32
    )

    def local_bunching(phase):
        harmonic_phase = HARM * phase
        cosine = jnp.cos(harmonic_phase)
        sine_part = jnp.sin(harmonic_phase)
        sums = jnp.stack(
            [
                jnp.sum(select * (weighted * cosine)[None, :], axis=1),
                jnp.sum(select * (-weighted * sine_part)[None, :], axis=1),
            ]
        )
        return cosine, sine_part, sums

    cosine0, sine0, sums0 = local_bunching(got_phase)
    sums_row = jnp.pad(sums0.reshape(1, 2 * SL_DEV), ((0, 7), (0, grid_y - 2 * SL_DEV)))
    stacked = jnp.concatenate([partial, sums_row])
    chunk_rows = -(-stacked.shape[0] // (splits * 8)) * 8
    stacked = jnp.pad(stacked, ((0, chunk_rows * splits - stacked.shape[0]), (0, 0)))
    summed = pb_sum(stacked, "pb")
    density = summed[:density_rows].reshape(SL_DEV, grid_x, grid_y)
    bunching0 = summed[density_rows, : 2 * SL_DEV].reshape(2, SL_DEV)

    below = shifted(density[SL_DEV - 1], "ta", 1)
    above = shifted(density[0], "ta", -1)
    empty = jnp.zeros((1, grid_x, grid_y), jnp.float32)
    force_map = stencil(jnp.concatenate([empty, density, empty]), along_coeff, across_coeff)

    force_rows = force_map.reshape(SL_DEV * grid_x, grid_y)
    force_hi = lax.reduce_precision(force_rows, exponent_bits=8, mantissa_bits=7)
    force_parts = jnp.concatenate(
        [force_hi.astype(jnp.bfloat16), (force_rows - force_hi).astype(jnp.bfloat16)], axis=1
    )
    pick_row = (row_key[:, None] == jnp.arange(SL_DEV * grid_x, dtype=jnp.int32)[None, :]).astype(
        jnp.bfloat16
    )
    picked = jnp.dot(pick_row, force_parts, preferred_element_type=jnp.float32)
    picked = picked[:, :grid_y] + picked[:, grid_y:]
    pick_col = got_y[:, None] == jnp.arange(grid_y, dtype=jnp.int32)[None, :]
    force_here = jnp.sum(jnp.where(pick_col, picked, 0.0), axis=1)
    halo_force = jnp.concatenate([-along_coeff * below, along_coeff * above]).reshape(
        2 * grid_x, grid_y
    )
    halo_hi = lax.reduce_precision(halo_force, exponent_bits=8, mantissa_bits=7)
    halo_parts = jnp.concatenate(
        [halo_hi.astype(jnp.bfloat16), (halo_force - halo_hi).astype(jnp.bfloat16)], axis=1
    )
    halo_key = jnp.where(
        got_slice == 0, got_x, jnp.where(got_slice == SL_DEV - 1, got_x + grid_x, -1)
    )
    pick_halo = (halo_key[:, None] == jnp.arange(2 * grid_x, dtype=jnp.int32)[None, :]).astype(
        jnp.bfloat16
    )
    halo_picked = jnp.dot(pick_halo, halo_parts, preferred_element_type=jnp.float32)
    halo_picked = halo_picked[:, :grid_y] + halo_picked[:, grid_y:]
    halo_here = jnp.sum(jnp.where(pick_col, halo_picked, 0.0), axis=1)
    kicked = got_energy + (force_here + halo_here)

    couple = 1.0 / math.sqrt(splits * PS_DEV)
    radiation = jnp.zeros((2, SL_DEV), jnp.float32)
    for period in range(PERIODS):
        if period == 0:
            cosine, sine_part, bunching = cosine0, sine0, bunching0
        else:
            cosine, sine_part, local_sums = local_bunching(got_phase)
            bunching = pb_sum_small(local_sums, "pb")
        radiation = radiation + couple * bunching
        real_here = jnp.sum(select * radiation[0][:, None], axis=0)
        imag_here = jnp.sum(select * radiation[1][:, None], axis=0)
        kicked = kicked + KICK_GAIN * profile * (real_here * cosine - imag_here * sine_part)
        got_phase = got_phase + SLIP_GAIN * kicked
        incoming = shifted(radiation[:, -1:], "ta", 1)
        radiation = jnp.concatenate([incoming, radiation[:, :-1]], axis=1)
    filled = arrived_weight > 0
    result = jnp.stack([jnp.where(filled, got_phase, 0.0), jnp.where(filled, kicked, 0.0)])
    return (result, radiation)


def solution(mesh):
    return jax.shard_map(
        body,
        mesh=mesh,
        in_specs=(
            P(None, ("ta", "pb")),
            P(("ta", "pb")),
            P(("ta", "pb")),
            P(("ta", "pb"), None),
            P(("ta", "pb")),
            P(),
            P(),
            P(),
            P(),
            P(),
            P(),
        ),
        out_specs=(P(None, ("ta", "pb")), P(None, "ta")),
        check_vma=False,
    )
```

```python
import math

import jax
import jax.numpy as jnp
from jax import lax
from jax.sharding import PartitionSpec as P

SL_DEV = 4
PS_DEV = 1024
HARM = 48
PERIODS = 2


DISPERSION = 3.0
LASER_GAIN = 1.0
KICK_GAIN = 0.5
SLIP_GAIN = 0.05


def shifted(value, axis, steps):
    count = lax.axis_size(axis)
    leading, last = (max(0, -steps), min(count, count - steps))
    return lax.ppermute(value, axis, [(source, source + steps) for source in range(leading, last)])


def lookup(values_table, positions):
    matches = positions[None, :] == jnp.arange(values_table.shape[0], dtype=jnp.int32)[:, None]
    return jnp.sum(jnp.where(matches, values_table[:, None], 0.0), axis=0)


def split3(x):
    hi = lax.reduce_precision(x, exponent_bits=8, mantissa_bits=7)
    rest = x - hi
    mid = lax.reduce_precision(rest, exponent_bits=8, mantissa_bits=7)
    lo = rest - mid
    return [part.astype(jnp.bfloat16) for part in (hi, mid, lo)]


def arrival_slots(to_group):
    groups, count = to_group.shape
    block_size = math.gcd(count, 512)
    turn_count = count // block_size
    onehot = to_group.astype(jnp.bfloat16).reshape(groups, turn_count, block_size)
    earlier = (jnp.arange(block_size)[:, None] > jnp.arange(block_size)[None, :]).astype(
        jnp.bfloat16
    )
    within = jnp.einsum("gtj,ij->gti", onehot, earlier, preferred_element_type=jnp.float32)
    rows_f = onehot.astype(jnp.float32)
    per_turn = jnp.sum(rows_f, axis=2)
    offsets = jnp.cumsum(per_turn, axis=1) - per_turn
    arrival = jnp.sum((within + offsets[:, :, None]) * rows_f, axis=0)
    return arrival.reshape(count).astype(jnp.int32)


def deposit_rows(weight_bf16, row_key, col, targets, grid_y):
    left = jnp.where(
        row_key[None, :] == targets[:, None], weight_bf16[None, :], jnp.zeros((), jnp.bfloat16)
    )
    right = (jnp.arange(grid_y, dtype=jnp.int32)[:, None] == col[None, :]).astype(jnp.bfloat16)
    return lax.dot_general(
        left, right, (((1,), (1,)), ((), ())), preferred_element_type=jnp.float32
    )


def pb_sum(rows, axis):
    count = lax.axis_size(axis)
    chunks = rows.reshape((count, -1) + rows.shape[1:])
    mine = jnp.sum(lax.all_to_all(chunks, axis, 0, 0, tiled=True), axis=0)
    every = lax.all_to_all(jnp.broadcast_to(mine[None], chunks.shape), axis, 0, 0, tiled=True)
    return every.reshape(rows.shape)


def pb_sum_small(value, axis):
    count = lax.axis_size(axis)
    spread = jnp.broadcast_to(value[None], (count,) + value.shape)
    return jnp.sum(lax.all_to_all(spread, axis, 0, 0, tiled=True), axis=0)


def stencil(extended, coeff_long, coeff_cross):
    centre = extended[1:-1]
    along_diff = extended[2:] - extended[:-2]
    padded_x = jnp.pad(centre, ((0, 0), (1, 1), (0, 0)))
    across = padded_x[:, 2:, :] + padded_x[:, :-2, :]
    padded_y = jnp.pad(centre, ((0, 0), (0, 0), (1, 1)))
    upper_y = padded_y[:, :, 2:]
    lower_y = padded_y[:, :, :-2]
    return coeff_long[None] * along_diff + coeff_cross[None] * (
        4.0 * centre - across - upper_y - lower_y
    )


def body(
    particles,
    weights,
    cell_index,
    target_group,
    target_slice,
    laser_x,
    laser_y,
    mode_x,
    mode_y,
    along_coeff,
    across_coeff,
):
    groups = lax.axis_size("ta")
    splits = lax.axis_size("pb")
    grid_x = laser_x.shape[0]
    grid_y = laser_y.shape[0]
    cell_count = grid_x * grid_y
    per_device = particles.shape[1]
    capacity = 2 * per_device // groups
    slot_count = groups * capacity
    row_x = cell_index // grid_y
    row_y = cell_index % grid_y
    energy = particles[1] + LASER_GAIN * lookup(laser_x, row_x) * lookup(laser_y, row_y) * jnp.sin(
        particles[0]
    )
    phases = particles[0] + DISPERSION * energy
    destination = target_group.reshape(1, per_device)
    to_group = destination == jnp.arange(groups, dtype=jnp.int32)[:, None]
    arrival = arrival_slots(to_group)

    values = jnp.stack(
        [
            phases,
            energy,
            weights.astype(jnp.float32),
            (target_slice * cell_count + cell_index).astype(jnp.float32),
        ]
    )
    value_count = values.shape[0]
    parts = split3(values)
    left = jnp.concatenate(
        [
            jnp.where(to_group[None], part[:, None, :], jnp.zeros((), jnp.bfloat16)).reshape(
                value_count * groups, per_device
            )
            for part in parts
        ]
    )
    to_slot = (arrival[:, None] == jnp.arange(capacity, dtype=jnp.int32)[None, :]).astype(
        jnp.bfloat16
    )
    placed = jnp.dot(left, to_slot, preferred_element_type=jnp.float32)
    rows = value_count * groups
    send = (placed[:rows] + placed[rows : 2 * rows]) + placed[2 * rows :]
    got = lax.all_to_all(
        send.reshape(value_count, groups, capacity), "ta", split_axis=1, concat_axis=1, tiled=True
    ).reshape(value_count, slot_count)

    got_phase = got[0]
    got_energy = got[1]
    arrived_weight = got[2]
    combined = got[3].astype(jnp.int32)
    got_slice = combined // cell_count
    got_cell = combined % cell_count
    got_x = got_cell // grid_y
    got_y = got_cell % grid_y
    row_key = got_slice * grid_x + got_x
    weight_bf16 = arrived_weight.astype(jnp.bfloat16)

    density_rows = SL_DEV * grid_x
    partial = deposit_rows(
        weight_bf16, row_key, got_y, jnp.arange(density_rows, dtype=jnp.int32), grid_y
    )

    profile = lookup(mode_x, got_x) * lookup(mode_y, got_y)
    weighted = arrived_weight * profile
    select = (got_slice[None, :] == jnp.arange(SL_DEV, dtype=jnp.int32)[:, None]).astype(
        jnp.float32
    )

    def local_bunching(phase):
        harmonic_phase = HARM * phase
        cosine = jnp.cos(harmonic_phase)
        sine_part = jnp.sin(harmonic_phase)
        sums = jnp.stack(
            [
                jnp.sum(select * (weighted * cosine)[None, :], axis=1),
                jnp.sum(select * (-weighted * sine_part)[None, :], axis=1),
            ]
        )
        return cosine, sine_part, sums

    cosine0, sine0, sums0 = local_bunching(got_phase)
    sums_row = jnp.pad(sums0.reshape(1, 2 * SL_DEV), ((0, 7), (0, grid_y - 2 * SL_DEV)))
    stacked = jnp.concatenate([partial, sums_row])
    chunk_rows = -(-stacked.shape[0] // (splits * 8)) * 8
    stacked = jnp.pad(stacked, ((0, chunk_rows * splits - stacked.shape[0]), (0, 0)))
    summed = pb_sum(stacked, "pb")
    density = summed[:density_rows].reshape(SL_DEV, grid_x, grid_y)
    bunching0 = summed[density_rows, : 2 * SL_DEV].reshape(2, SL_DEV)

    couple = 1.0 / math.sqrt(splits * PS_DEV)
    radiation0 = couple * bunching0
    last_row = jnp.pad(radiation0[:, -1:].reshape(1, 2), ((0, 7), (0, grid_y - 2)))
    halo_below = shifted(jnp.concatenate([density[SL_DEV - 1], last_row]), "ta", 1)
    above = shifted(density[0], "ta", -1)
    empty = jnp.zeros((1, grid_x, grid_y), jnp.float32)
    force_map = stencil(jnp.concatenate([empty, density, empty]), along_coeff, across_coeff)

    def pick(table, key, key_count):
        table_hi = lax.reduce_precision(table, exponent_bits=8, mantissa_bits=7)
        table_parts = jnp.concatenate(
            [table_hi.astype(jnp.bfloat16), (table - table_hi).astype(jnp.bfloat16)], axis=1
        ).T
        pick_row = (jnp.arange(key_count, dtype=jnp.int32)[:, None] == key[None, :]).astype(
            jnp.bfloat16
        )
        picked = jnp.dot(table_parts, pick_row, preferred_element_type=jnp.float32)
        picked = picked[:grid_y] + picked[grid_y:]
        return jnp.sum(jnp.where(pick_col, picked, 0.0), axis=0)

    pick_col = jnp.arange(grid_y, dtype=jnp.int32)[:, None] == got_y[None, :]
    force_here = pick(force_map.reshape(SL_DEV * grid_x, grid_y), row_key, SL_DEV * grid_x)
    below_density = halo_below[:grid_x]
    halo_force = jnp.concatenate([-along_coeff * below_density, along_coeff * above]).reshape(
        2 * grid_x, grid_y
    )
    halo_key = jnp.where(
        got_slice == 0, got_x, jnp.where(got_slice == SL_DEV - 1, got_x + grid_x, -1)
    )
    halo_here = pick(halo_force, halo_key, 2 * grid_x)
    kicked = got_energy + (force_here + halo_here)

    radiation = jnp.zeros((2, SL_DEV), jnp.float32)
    for period in range(PERIODS):
        if period == 0:
            cosine, sine_part = cosine0, sine0
            radiation = radiation + radiation0
        else:
            cosine, sine_part, local_sums = local_bunching(got_phase)
            bunching = pb_sum_small(local_sums, "pb")
            radiation = radiation + couple * bunching
        real_here = jnp.sum(select * radiation[0][:, None], axis=0)
        imag_here = jnp.sum(select * radiation[1][:, None], axis=0)
        kicked = kicked + KICK_GAIN * profile * (real_here * cosine - imag_here * sine_part)
        got_phase = got_phase + SLIP_GAIN * kicked
        if period == 0:
            incoming = halo_below[grid_x, :2].reshape(2, 1)
        else:
            incoming = shifted(radiation[:, -1:], "ta", 1)
        radiation = jnp.concatenate([incoming, radiation[:, :-1]], axis=1)
    filled = arrived_weight > 0
    result = jnp.stack([jnp.where(filled, got_phase, 0.0), jnp.where(filled, kicked, 0.0)])
    return (result, radiation)


def solution(mesh):
    return jax.shard_map(
        body,
        mesh=mesh,
        in_specs=(
            P(None, ("ta", "pb")),
            P(("ta", "pb")),
            P(("ta", "pb")),
            P(("ta", "pb"), None),
            P(("ta", "pb")),
            P(),
            P(),
            P(),
            P(),
            P(),
            P(),
        ),
        out_specs=(P(None, ("ta", "pb")), P(None, "ta")),
        check_vma=False,
    )
```

```python
import math

import jax
import jax.numpy as jnp
from jax import lax
from jax.sharding import PartitionSpec as P

SL_DEV = 4
PS_DEV = 1024
HARM = 48
PERIODS = 2


DISPERSION = 3.0
LASER_GAIN = 1.0
KICK_GAIN = 0.5
SLIP_GAIN = 0.05


def shifted(value, axis, steps):
    count = lax.axis_size(axis)
    leading, last = (max(0, -steps), min(count, count - steps))
    return lax.ppermute(value, axis, [(source, source + steps) for source in range(leading, last)])


def lookup(values_table, positions):
    matches = positions[None, :] == jnp.arange(values_table.shape[0], dtype=jnp.int32)[:, None]
    return jnp.sum(jnp.where(matches, values_table[:, None], 0.0), axis=0)


def split3(x):
    hi = lax.reduce_precision(x, exponent_bits=8, mantissa_bits=7)
    rest = x - hi
    mid = lax.reduce_precision(rest, exponent_bits=8, mantissa_bits=7)
    lo = rest - mid
    return [part.astype(jnp.bfloat16) for part in (hi, mid, lo)]


def arrival_slots(to_group):
    groups, count = to_group.shape
    block_size = math.gcd(count, 512)
    turn_count = count // block_size
    onehot = to_group.astype(jnp.bfloat16).reshape(groups, turn_count, block_size)
    earlier = (jnp.arange(block_size)[:, None] > jnp.arange(block_size)[None, :]).astype(
        jnp.bfloat16
    )
    within = jnp.einsum("gtj,ij->gti", onehot, earlier, preferred_element_type=jnp.float32)
    rows_f = onehot.astype(jnp.float32)
    per_turn = jnp.sum(rows_f, axis=2)
    offsets = jnp.cumsum(per_turn, axis=1) - per_turn
    arrival = jnp.sum((within + offsets[:, :, None]) * rows_f, axis=0)
    return arrival.reshape(count).astype(jnp.int32)


def deposit_rows(weight_bf16, row_key, col, targets, grid_y):
    left = jnp.where(
        row_key[None, :] == targets[:, None], weight_bf16[None, :], jnp.zeros((), jnp.bfloat16)
    )
    right = (jnp.arange(grid_y, dtype=jnp.int32)[:, None] == col[None, :]).astype(jnp.bfloat16)
    return lax.dot_general(
        left, right, (((1,), (1,)), ((), ())), preferred_element_type=jnp.float32
    )


def pb_sum(rows, axis):
    count = lax.axis_size(axis)
    chunks = rows.reshape((count, -1) + rows.shape[1:])
    mine = jnp.sum(lax.all_to_all(chunks, axis, 0, 0, tiled=True), axis=0)
    every = lax.all_to_all(jnp.broadcast_to(mine[None], chunks.shape), axis, 0, 0, tiled=True)
    return every.reshape(rows.shape)


def pb_sum_small(value, axis):
    count = lax.axis_size(axis)
    spread = jnp.broadcast_to(value[None], (count,) + value.shape)
    return jnp.sum(lax.all_to_all(spread, axis, 0, 0, tiled=True), axis=0)


def stencil(extended, coeff_long, coeff_cross):
    centre = extended[1:-1]
    along_diff = extended[2:] - extended[:-2]
    padded_x = jnp.pad(centre, ((0, 0), (1, 1), (0, 0)))
    across = padded_x[:, 2:, :] + padded_x[:, :-2, :]
    padded_y = jnp.pad(centre, ((0, 0), (0, 0), (1, 1)))
    upper_y = padded_y[:, :, 2:]
    lower_y = padded_y[:, :, :-2]
    return coeff_long[None] * along_diff + coeff_cross[None] * (
        4.0 * centre - across - upper_y - lower_y
    )


def body(
    particles,
    weights,
    cell_index,
    target_group,
    target_slice,
    laser_x,
    laser_y,
    mode_x,
    mode_y,
    along_coeff,
    across_coeff,
):
    groups = lax.axis_size("ta")
    splits = lax.axis_size("pb")
    grid_x = laser_x.shape[0]
    grid_y = laser_y.shape[0]
    cell_count = grid_x * grid_y
    per_device = particles.shape[1]
    capacity = 2 * per_device // groups
    slot_count = groups * capacity
    row_x = cell_index // grid_y
    row_y = cell_index % grid_y
    energy = particles[1] + LASER_GAIN * lookup(laser_x, row_x) * lookup(laser_y, row_y) * jnp.sin(
        particles[0]
    )
    phases = particles[0] + DISPERSION * energy
    destination = target_group.reshape(1, per_device)
    to_group = destination == jnp.arange(groups, dtype=jnp.int32)[:, None]
    arrival = arrival_slots(to_group)

    index_value = (target_slice * cell_count + cell_index).astype(jnp.float32)
    index_hi = lax.reduce_precision(index_value, exponent_bits=8, mantissa_bits=7)
    pieces = jnp.stack(
        split3(phases)
        + split3(energy)
        + [weights, index_hi.astype(jnp.bfloat16), (index_value - index_hi).astype(jnp.bfloat16)]
    )
    piece_count = pieces.shape[0]
    left = jnp.where(to_group[None], pieces[:, None, :], jnp.zeros((), jnp.bfloat16)).reshape(
        piece_count * groups, per_device
    )
    to_slot = (jnp.arange(capacity, dtype=jnp.int32)[:, None] == arrival[None, :]).astype(
        jnp.bfloat16
    )
    placed = lax.dot_general(
        left, to_slot, (((1,), (1,)), ((), ())), preferred_element_type=jnp.float32
    ).reshape(piece_count, groups, capacity)
    send = jnp.stack(
        [
            (placed[0] + placed[1]) + placed[2],
            (placed[3] + placed[4]) + placed[5],
            placed[6],
            placed[7] + placed[8],
        ]
    )
    value_count = send.shape[0]
    got = lax.all_to_all(
        send.reshape(value_count, groups, capacity), "ta", split_axis=1, concat_axis=1, tiled=True
    ).reshape(value_count, slot_count)

    got_phase = got[0]
    got_energy = got[1]
    arrived_weight = got[2]
    combined = got[3].astype(jnp.int32)
    got_slice = combined // cell_count
    got_cell = combined % cell_count
    got_x = got_cell // grid_y
    got_y = got_cell % grid_y
    row_key = got_slice * grid_x + got_x
    weight_bf16 = arrived_weight.astype(jnp.bfloat16)

    density_rows = SL_DEV * grid_x
    partial = deposit_rows(
        weight_bf16, row_key, got_y, jnp.arange(density_rows, dtype=jnp.int32), grid_y
    )

    profile = lookup(mode_x, got_x) * lookup(mode_y, got_y)
    weighted = arrived_weight * profile
    select = (got_slice[None, :] == jnp.arange(SL_DEV, dtype=jnp.int32)[:, None]).astype(
        jnp.float32
    )

    def local_bunching(phase):
        harmonic_phase = HARM * phase
        cosine = jnp.cos(harmonic_phase)
        sine_part = jnp.sin(harmonic_phase)
        sums = jnp.stack(
            [
                jnp.sum(select * (weighted * cosine)[None, :], axis=1),
                jnp.sum(select * (-weighted * sine_part)[None, :], axis=1),
            ]
        )
        return cosine, sine_part, sums

    cosine0, sine0, sums0 = local_bunching(got_phase)
    sums_row = jnp.pad(sums0.reshape(1, 2 * SL_DEV), ((0, 7), (0, grid_y - 2 * SL_DEV)))
    stacked = jnp.concatenate([partial, sums_row])
    chunk_rows = -(-stacked.shape[0] // (splits * 8)) * 8
    stacked = jnp.pad(stacked, ((0, chunk_rows * splits - stacked.shape[0]), (0, 0)))
    summed = pb_sum(stacked, "pb")
    density = summed[:density_rows].reshape(SL_DEV, grid_x, grid_y)
    bunching0 = summed[density_rows, : 2 * SL_DEV].reshape(2, SL_DEV)

    couple = 1.0 / math.sqrt(splits * PS_DEV)
    radiation0 = couple * bunching0
    last_row = jnp.pad(radiation0[:, -1:].reshape(1, 2), ((0, 7), (0, grid_y - 2)))
    halo_below = shifted(jnp.concatenate([density[SL_DEV - 1], last_row]), "ta", 1)
    above = shifted(density[0], "ta", -1)
    empty = jnp.zeros((1, grid_x, grid_y), jnp.float32)
    force_map = stencil(jnp.concatenate([empty, density, empty]), along_coeff, across_coeff)

    def pick(table, key, key_count):
        table_hi = lax.reduce_precision(table, exponent_bits=8, mantissa_bits=7)
        table_parts = jnp.concatenate(
            [table_hi.astype(jnp.bfloat16), (table - table_hi).astype(jnp.bfloat16)], axis=1
        ).T
        pick_row = (jnp.arange(key_count, dtype=jnp.int32)[:, None] == key[None, :]).astype(
            jnp.bfloat16
        )
        picked = jnp.dot(table_parts, pick_row, preferred_element_type=jnp.float32)
        picked = picked[:grid_y] + picked[grid_y:]
        return jnp.sum(jnp.where(pick_col, picked, 0.0), axis=0)

    pick_col = jnp.arange(grid_y, dtype=jnp.int32)[:, None] == got_y[None, :]
    force_here = pick(force_map.reshape(SL_DEV * grid_x, grid_y), row_key, SL_DEV * grid_x)
    below_density = halo_below[:grid_x]
    halo_force = jnp.concatenate([-along_coeff * below_density, along_coeff * above]).reshape(
        2 * grid_x, grid_y
    )
    halo_key = jnp.where(
        got_slice == 0, got_x, jnp.where(got_slice == SL_DEV - 1, got_x + grid_x, -1)
    )
    halo_here = pick(halo_force, halo_key, 2 * grid_x)
    kicked = got_energy + (force_here + halo_here)

    radiation = jnp.zeros((2, SL_DEV), jnp.float32)
    for period in range(PERIODS):
        if period == 0:
            cosine, sine_part = cosine0, sine0
            radiation = radiation + radiation0
        else:
            cosine, sine_part, local_sums = local_bunching(got_phase)
            bunching = pb_sum_small(local_sums, "pb")
            radiation = radiation + couple * bunching
        real_here = jnp.sum(select * radiation[0][:, None], axis=0)
        imag_here = jnp.sum(select * radiation[1][:, None], axis=0)
        kicked = kicked + KICK_GAIN * profile * (real_here * cosine - imag_here * sine_part)
        got_phase = got_phase + SLIP_GAIN * kicked
        if period == 0:
            incoming = halo_below[grid_x, :2].reshape(2, 1)
        else:
            incoming = shifted(radiation[:, -1:], "ta", 1)
        radiation = jnp.concatenate([incoming, radiation[:, :-1]], axis=1)
    filled = arrived_weight > 0
    result = jnp.stack([jnp.where(filled, got_phase, 0.0), jnp.where(filled, kicked, 0.0)])
    return (result, radiation)


def solution(mesh):
    return jax.shard_map(
        body,
        mesh=mesh,
        in_specs=(
            P(None, ("ta", "pb")),
            P(("ta", "pb")),
            P(("ta", "pb")),
            P(("ta", "pb"), None),
            P(("ta", "pb")),
            P(),
            P(),
            P(),
            P(),
            P(),
            P(),
        ),
        out_specs=(P(None, ("ta", "pb")), P(None, "ta")),
        check_vma=False,
    )
```

```python
import math

import jax
import jax.numpy as jnp
from jax import lax
from jax.sharding import PartitionSpec as P

SL_DEV = 4
PS_DEV = 1024
HARM = 48
PERIODS = 2


DISPERSION = 3.0
LASER_GAIN = 1.0
KICK_GAIN = 0.5
SLIP_GAIN = 0.05


def shifted(value, axis, steps):
    count = lax.axis_size(axis)
    leading, last = (max(0, -steps), min(count, count - steps))
    return lax.ppermute(value, axis, [(source, source + steps) for source in range(leading, last)])


def lookup(values_table, positions):
    matches = positions[None, :] == jnp.arange(values_table.shape[0], dtype=jnp.int32)[:, None]
    return jnp.sum(jnp.where(matches, values_table[:, None], 0.0), axis=0)


def split3(x):
    hi = lax.reduce_precision(x, exponent_bits=8, mantissa_bits=7)
    rest = x - hi
    mid = lax.reduce_precision(rest, exponent_bits=8, mantissa_bits=7)
    lo = rest - mid
    return [part.astype(jnp.bfloat16) for part in (hi, mid, lo)]


def arrival_slots(to_group):
    groups, count = to_group.shape
    block_size = math.gcd(count, 512)
    turn_count = count // block_size
    onehot = to_group.astype(jnp.bfloat16).reshape(groups, turn_count, block_size)
    earlier = (jnp.arange(block_size)[:, None] > jnp.arange(block_size)[None, :]).astype(
        jnp.bfloat16
    )
    within = jnp.einsum("gtj,ij->gti", onehot, earlier, preferred_element_type=jnp.float32)
    rows_f = onehot.astype(jnp.float32)
    per_turn = jnp.sum(rows_f, axis=2)
    offsets = jnp.cumsum(per_turn, axis=1) - per_turn
    arrival = jnp.sum((within + offsets[:, :, None]) * rows_f, axis=0)
    return arrival.reshape(count).astype(jnp.int32)


def deposit_rows(weight_bf16, row_key, col, targets, grid_y):
    left = jnp.where(
        row_key[None, :] == targets[:, None], weight_bf16[None, :], jnp.zeros((), jnp.bfloat16)
    )
    right = (jnp.arange(grid_y, dtype=jnp.int32)[:, None] == col[None, :]).astype(jnp.bfloat16)
    return lax.dot_general(
        left, right, (((1,), (1,)), ((), ())), preferred_element_type=jnp.float32
    )


def pb_sum(rows, axis):
    count = lax.axis_size(axis)
    chunks = rows.reshape((count, -1) + rows.shape[1:])
    mine = jnp.sum(lax.all_to_all(chunks, axis, 0, 0, tiled=True), axis=0)
    every = lax.all_to_all(jnp.broadcast_to(mine[None], chunks.shape), axis, 0, 0, tiled=True)
    return every.reshape(rows.shape)


def pb_sum_small(value, axis):
    count = lax.axis_size(axis)
    spread = jnp.broadcast_to(value[None], (count,) + value.shape)
    return jnp.sum(lax.all_to_all(spread, axis, 0, 0, tiled=True), axis=0)


def stencil(extended, coeff_long, coeff_cross):
    centre = extended[1:-1]
    along_diff = extended[2:] - extended[:-2]
    padded_x = jnp.pad(centre, ((0, 0), (1, 1), (0, 0)))
    across = padded_x[:, 2:, :] + padded_x[:, :-2, :]
    padded_y = jnp.pad(centre, ((0, 0), (0, 0), (1, 1)))
    upper_y = padded_y[:, :, 2:]
    lower_y = padded_y[:, :, :-2]
    return coeff_long[None] * along_diff + coeff_cross[None] * (
        4.0 * centre - across - upper_y - lower_y
    )


def body(
    particles,
    weights,
    cell_index,
    target_group,
    target_slice,
    laser_x,
    laser_y,
    mode_x,
    mode_y,
    along_coeff,
    across_coeff,
):
    groups = lax.axis_size("ta")
    splits = lax.axis_size("pb")
    grid_x = laser_x.shape[0]
    grid_y = laser_y.shape[0]
    cell_count = grid_x * grid_y
    per_device = particles.shape[1]
    capacity = 2 * per_device // groups
    slot_count = groups * capacity
    row_x = cell_index // grid_y
    row_y = cell_index % grid_y
    energy = particles[1] + LASER_GAIN * lookup(laser_x, row_x) * lookup(laser_y, row_y) * jnp.sin(
        particles[0]
    )
    phases = particles[0] + DISPERSION * energy
    destination = target_group.reshape(1, per_device)
    to_group = destination == jnp.arange(groups, dtype=jnp.int32)[:, None]
    arrival = arrival_slots(to_group)

    values = jnp.stack(
        [
            phases,
            energy,
            weights.astype(jnp.float32),
            (target_slice * cell_count + cell_index).astype(jnp.float32),
        ]
    )
    value_count = values.shape[0]
    parts = split3(values)
    left = jnp.concatenate(
        [
            jnp.where(to_group[None], part[:, None, :], jnp.zeros((), jnp.bfloat16)).reshape(
                value_count * groups, per_device
            )
            for part in parts
        ]
    )
    to_slot = (arrival[:, None] == jnp.arange(capacity, dtype=jnp.int32)[None, :]).astype(
        jnp.bfloat16
    )
    placed = jnp.dot(left, to_slot, preferred_element_type=jnp.float32)
    rows = value_count * groups
    send = (placed[:rows] + placed[rows : 2 * rows]) + placed[2 * rows :]
    got = lax.all_to_all(
        send.reshape(value_count, groups, capacity), "ta", split_axis=1, concat_axis=1, tiled=True
    ).reshape(value_count, slot_count)

    got_phase = got[0]
    got_energy = got[1]
    arrived_weight = got[2]
    combined = got[3].astype(jnp.int32)
    got_slice = combined // cell_count
    got_cell = combined % cell_count
    got_x = got_cell // grid_y
    got_y = got_cell % grid_y
    row_key = got_slice * grid_x + got_x
    weight_bf16 = arrived_weight.astype(jnp.bfloat16)

    density_rows = SL_DEV * grid_x
    partial = deposit_rows(
        weight_bf16, row_key, got_y, jnp.arange(density_rows, dtype=jnp.int32), grid_y
    )

    profile = lookup(mode_x, got_x) * lookup(mode_y, got_y)
    weighted = arrived_weight * profile
    select = (got_slice[None, :] == jnp.arange(SL_DEV, dtype=jnp.int32)[:, None]).astype(
        jnp.float32
    )

    def local_bunching(phase):
        harmonic_phase = HARM * phase
        cosine = jnp.cos(harmonic_phase)
        sine_part = jnp.sin(harmonic_phase)
        sums = jnp.stack(
            [
                jnp.sum(select * (weighted * cosine)[None, :], axis=1),
                jnp.sum(select * (-weighted * sine_part)[None, :], axis=1),
            ]
        )
        return cosine, sine_part, sums

    cosine0, sine0, sums0 = local_bunching(got_phase)
    lanes = -(-(grid_y + 2 * SL_DEV) // 128) * 128
    chunk_rows = -(-density_rows // (splits * 8)) * 8
    side = jnp.pad(
        sums0.reshape(1, 2 * SL_DEV),
        ((0, chunk_rows * splits - 1), (0, lanes - grid_y - 2 * SL_DEV)),
    )
    stacked = jnp.pad(partial, ((0, chunk_rows * splits - density_rows), (0, 0)))
    stacked = jnp.concatenate([stacked, side], axis=1)
    summed = pb_sum(stacked, "pb")
    density = summed[:density_rows, :grid_y].reshape(SL_DEV, grid_x, grid_y)
    bunching0 = summed[0, grid_y : grid_y + 2 * SL_DEV].reshape(2, SL_DEV)

    couple = 1.0 / math.sqrt(splits * PS_DEV)
    radiation0 = couple * bunching0
    last_row = jnp.pad(radiation0[:, -1:].reshape(1, 2), ((0, 7), (0, grid_y - 2)))
    halo_below = shifted(jnp.concatenate([density[SL_DEV - 1], last_row]), "ta", 1)
    above = shifted(density[0], "ta", -1)
    empty = jnp.zeros((1, grid_x, grid_y), jnp.float32)
    force_map = stencil(jnp.concatenate([empty, density, empty]), along_coeff, across_coeff)

    def pick(table, key, key_count):
        table_hi = lax.reduce_precision(table, exponent_bits=8, mantissa_bits=7)
        table_parts = jnp.concatenate(
            [table_hi.astype(jnp.bfloat16), (table - table_hi).astype(jnp.bfloat16)], axis=1
        ).T
        pick_row = (jnp.arange(key_count, dtype=jnp.int32)[:, None] == key[None, :]).astype(
            jnp.bfloat16
        )
        picked = jnp.dot(table_parts, pick_row, preferred_element_type=jnp.float32)
        picked = picked[:grid_y] + picked[grid_y:]
        return jnp.sum(jnp.where(pick_col, picked, 0.0), axis=0)

    pick_col = jnp.arange(grid_y, dtype=jnp.int32)[:, None] == got_y[None, :]
    force_here = pick(force_map.reshape(SL_DEV * grid_x, grid_y), row_key, SL_DEV * grid_x)
    below_density = halo_below[:grid_x]
    halo_force = jnp.concatenate([-along_coeff * below_density, along_coeff * above]).reshape(
        2 * grid_x, grid_y
    )
    halo_key = jnp.where(
        got_slice == 0, got_x, jnp.where(got_slice == SL_DEV - 1, got_x + grid_x, -1)
    )
    halo_here = pick(halo_force, halo_key, 2 * grid_x)
    kicked = got_energy + (force_here + halo_here)

    radiation = jnp.zeros((2, SL_DEV), jnp.float32)
    for period in range(PERIODS):
        if period == 0:
            cosine, sine_part = cosine0, sine0
            radiation = radiation + radiation0
        else:
            cosine, sine_part, local_sums = local_bunching(got_phase)
            bunching = pb_sum_small(local_sums, "pb")
            radiation = radiation + couple * bunching
        real_here = jnp.sum(select * radiation[0][:, None], axis=0)
        imag_here = jnp.sum(select * radiation[1][:, None], axis=0)
        kicked = kicked + KICK_GAIN * profile * (real_here * cosine - imag_here * sine_part)
        got_phase = got_phase + SLIP_GAIN * kicked
        if period == 0:
            incoming = halo_below[grid_x, :2].reshape(2, 1)
        else:
            incoming = shifted(radiation[:, -1:], "ta", 1)
        radiation = jnp.concatenate([incoming, radiation[:, :-1]], axis=1)
    filled = arrived_weight > 0
    result = jnp.stack([jnp.where(filled, got_phase, 0.0), jnp.where(filled, kicked, 0.0)])
    return (result, radiation)


def solution(mesh):
    return jax.shard_map(
        body,
        mesh=mesh,
        in_specs=(
            P(None, ("ta", "pb")),
            P(("ta", "pb")),
            P(("ta", "pb")),
            P(("ta", "pb"), None),
            P(("ta", "pb")),
            P(),
            P(),
            P(),
            P(),
            P(),
            P(),
        ),
        out_specs=(P(None, ("ta", "pb")), P(None, "ta")),
        check_vma=False,
    )
```

```python
import math

import jax
import jax.numpy as jnp
from jax import lax
from jax.sharding import PartitionSpec as P

SL_DEV = 4
PS_DEV = 1024
HARM = 48
PERIODS = 2


DISPERSION = 3.0
LASER_GAIN = 1.0
KICK_GAIN = 0.5
SLIP_GAIN = 0.05


def shifted(value, axis, steps):
    count = lax.axis_size(axis)
    leading, last = (max(0, -steps), min(count, count - steps))
    return lax.ppermute(value, axis, [(source, source + steps) for source in range(leading, last)])


def lookup(values_table, positions):
    matches = positions[None, :] == jnp.arange(values_table.shape[0], dtype=jnp.int32)[:, None]
    return jnp.sum(jnp.where(matches, values_table[:, None], 0.0), axis=0)


def split3(x):
    hi = lax.reduce_precision(x, exponent_bits=8, mantissa_bits=7)
    rest = x - hi
    mid = lax.reduce_precision(rest, exponent_bits=8, mantissa_bits=7)
    lo = rest - mid
    return [part.astype(jnp.bfloat16) for part in (hi, mid, lo)]


def arrival_slots(to_group):
    groups, count = to_group.shape
    block_size = math.gcd(count, 512)
    turn_count = count // block_size
    onehot = to_group.astype(jnp.bfloat16).reshape(groups, turn_count, block_size)
    earlier = (jnp.arange(block_size)[:, None] > jnp.arange(block_size)[None, :]).astype(
        jnp.bfloat16
    )
    within = jnp.einsum("gtj,ij->gti", onehot, earlier, preferred_element_type=jnp.float32)
    rows_f = onehot.astype(jnp.float32)
    per_turn = jnp.sum(rows_f, axis=2)
    offsets = jnp.cumsum(per_turn, axis=1) - per_turn
    arrival = jnp.sum((within + offsets[:, :, None]) * rows_f, axis=0)
    return arrival.reshape(count).astype(jnp.int32)


def deposit_rows(weight_bf16, row_key, col, targets, grid_y):
    left = jnp.where(
        row_key[None, :] == targets[:, None], weight_bf16[None, :], jnp.zeros((), jnp.bfloat16)
    )
    right = (jnp.arange(grid_y, dtype=jnp.int32)[:, None] == col[None, :]).astype(jnp.bfloat16)
    return lax.dot_general(
        left, right, (((1,), (1,)), ((), ())), preferred_element_type=jnp.float32
    )


def pb_sum(rows, axis):
    count = lax.axis_size(axis)
    chunks = rows.reshape((count, -1) + rows.shape[1:])
    mine = jnp.sum(lax.all_to_all(chunks, axis, 0, 0, tiled=True), axis=0)
    every = lax.all_to_all(jnp.broadcast_to(mine[None], chunks.shape), axis, 0, 0, tiled=True)
    return every.reshape(rows.shape)


def pb_sum_small(value, axis):
    count = lax.axis_size(axis)
    spread = jnp.broadcast_to(value[None], (count,) + value.shape)
    return jnp.sum(lax.all_to_all(spread, axis, 0, 0, tiled=True), axis=0)


def stencil(extended, coeff_long, coeff_cross):
    centre = extended[1:-1]
    along_diff = extended[2:] - extended[:-2]
    padded_x = jnp.pad(centre, ((0, 0), (1, 1), (0, 0)))
    across = padded_x[:, 2:, :] + padded_x[:, :-2, :]
    padded_y = jnp.pad(centre, ((0, 0), (0, 0), (1, 1)))
    upper_y = padded_y[:, :, 2:]
    lower_y = padded_y[:, :, :-2]
    return coeff_long[None] * along_diff + coeff_cross[None] * (
        4.0 * centre - across - upper_y - lower_y
    )


def body(
    particles,
    weights,
    cell_index,
    target_group,
    target_slice,
    laser_x,
    laser_y,
    mode_x,
    mode_y,
    along_coeff,
    across_coeff,
):
    groups = lax.axis_size("ta")
    splits = lax.axis_size("pb")
    grid_x = laser_x.shape[0]
    grid_y = laser_y.shape[0]
    cell_count = grid_x * grid_y
    per_device = particles.shape[1]
    capacity = 2 * per_device // groups
    slot_count = groups * capacity
    row_x = cell_index // grid_y
    row_y = cell_index % grid_y
    energy = particles[1] + LASER_GAIN * lookup(laser_x, row_x) * lookup(laser_y, row_y) * jnp.sin(
        particles[0]
    )
    phases = particles[0] + DISPERSION * energy
    destination = target_group.reshape(1, per_device)
    to_group = lax.optimization_barrier(destination == jnp.arange(groups, dtype=jnp.int32)[:, None])
    arrival = arrival_slots(to_group)

    values = jnp.stack(
        [
            phases,
            energy,
            weights.astype(jnp.float32),
            (target_slice * cell_count + cell_index).astype(jnp.float32),
        ]
    )
    value_count = values.shape[0]
    parts = split3(values)
    left = jnp.concatenate(
        [
            jnp.where(to_group[None], part[:, None, :], jnp.zeros((), jnp.bfloat16)).reshape(
                value_count * groups, per_device
            )
            for part in parts
        ]
    )
    to_slot = (arrival[:, None] == jnp.arange(capacity, dtype=jnp.int32)[None, :]).astype(
        jnp.bfloat16
    )
    placed = jnp.dot(left, to_slot, preferred_element_type=jnp.float32)
    rows = value_count * groups
    send = (placed[:rows] + placed[rows : 2 * rows]) + placed[2 * rows :]
    got = lax.all_to_all(
        send.reshape(value_count, groups, capacity), "ta", split_axis=1, concat_axis=1, tiled=True
    ).reshape(value_count, slot_count)

    got_phase = got[0]
    got_energy = got[1]
    arrived_weight = got[2]
    combined = got[3].astype(jnp.int32)
    got_slice = combined // cell_count
    got_cell = combined % cell_count
    got_x = got_cell // grid_y
    got_y = got_cell % grid_y
    row_key = got_slice * grid_x + got_x
    weight_bf16 = arrived_weight.astype(jnp.bfloat16)

    density_rows = SL_DEV * grid_x
    partial = deposit_rows(
        weight_bf16, row_key, got_y, jnp.arange(density_rows, dtype=jnp.int32), grid_y
    )

    profile = lookup(mode_x, got_x) * lookup(mode_y, got_y)
    weighted = arrived_weight * profile
    select = (got_slice[None, :] == jnp.arange(SL_DEV, dtype=jnp.int32)[:, None]).astype(
        jnp.float32
    )

    def local_bunching(phase):
        harmonic_phase = HARM * phase
        cosine = jnp.cos(harmonic_phase)
        sine_part = jnp.sin(harmonic_phase)
        sums = jnp.stack(
            [
                jnp.sum(select * (weighted * cosine)[None, :], axis=1),
                jnp.sum(select * (-weighted * sine_part)[None, :], axis=1),
            ]
        )
        return cosine, sine_part, sums

    cosine0, sine0, sums0 = local_bunching(got_phase)
    lanes = -(-(grid_y + 2 * SL_DEV) // 128) * 128
    chunk_rows = -(-density_rows // (splits * 8)) * 8
    side = jnp.pad(
        sums0.reshape(1, 2 * SL_DEV),
        ((0, chunk_rows * splits - 1), (0, lanes - grid_y - 2 * SL_DEV)),
    )
    stacked = jnp.pad(partial, ((0, chunk_rows * splits - density_rows), (0, 0)))
    stacked = jnp.concatenate([stacked, side], axis=1)
    summed = pb_sum(stacked, "pb")
    density = summed[:density_rows, :grid_y].reshape(SL_DEV, grid_x, grid_y)
    bunching0 = summed[0, grid_y : grid_y + 2 * SL_DEV].reshape(2, SL_DEV)

    couple = 1.0 / math.sqrt(splits * PS_DEV)
    radiation0 = couple * bunching0
    last_row = jnp.pad(radiation0[:, -1:].reshape(1, 2), ((0, 7), (0, grid_y - 2)))
    halo_below = shifted(jnp.concatenate([density[SL_DEV - 1], last_row]), "ta", 1)
    above = shifted(density[0], "ta", -1)
    empty = jnp.zeros((1, grid_x, grid_y), jnp.float32)
    force_map = stencil(jnp.concatenate([empty, density, empty]), along_coeff, across_coeff)

    def pick(table, key, key_count):
        table_hi = lax.reduce_precision(table, exponent_bits=8, mantissa_bits=7)
        table_parts = jnp.concatenate(
            [table_hi.astype(jnp.bfloat16), (table - table_hi).astype(jnp.bfloat16)], axis=1
        ).T
        pick_row = (jnp.arange(key_count, dtype=jnp.int32)[:, None] == key[None, :]).astype(
            jnp.bfloat16
        )
        picked = jnp.dot(table_parts, pick_row, preferred_element_type=jnp.float32)
        picked = picked[:grid_y] + picked[grid_y:]
        return jnp.sum(jnp.where(pick_col, picked, 0.0), axis=0)

    pick_col = jnp.arange(grid_y, dtype=jnp.int32)[:, None] == got_y[None, :]
    force_here = pick(force_map.reshape(SL_DEV * grid_x, grid_y), row_key, SL_DEV * grid_x)
    below_density = halo_below[:grid_x]
    halo_force = jnp.concatenate([-along_coeff * below_density, along_coeff * above]).reshape(
        2 * grid_x, grid_y
    )
    halo_key = jnp.where(
        got_slice == 0, got_x, jnp.where(got_slice == SL_DEV - 1, got_x + grid_x, -1)
    )
    halo_here = pick(halo_force, halo_key, 2 * grid_x)
    kicked = got_energy + (force_here + halo_here)

    radiation = jnp.zeros((2, SL_DEV), jnp.float32)
    for period in range(PERIODS):
        if period == 0:
            cosine, sine_part = cosine0, sine0
            radiation = radiation + radiation0
        else:
            cosine, sine_part, local_sums = local_bunching(got_phase)
            bunching = pb_sum_small(local_sums, "pb")
            radiation = radiation + couple * bunching
        real_here = jnp.sum(select * radiation[0][:, None], axis=0)
        imag_here = jnp.sum(select * radiation[1][:, None], axis=0)
        kicked = kicked + KICK_GAIN * profile * (real_here * cosine - imag_here * sine_part)
        got_phase = got_phase + SLIP_GAIN * kicked
        if period == 0:
            incoming = halo_below[grid_x, :2].reshape(2, 1)
        else:
            incoming = shifted(radiation[:, -1:], "ta", 1)
        radiation = jnp.concatenate([incoming, radiation[:, :-1]], axis=1)
    filled = arrived_weight > 0
    result = jnp.stack([jnp.where(filled, got_phase, 0.0), jnp.where(filled, kicked, 0.0)])
    return (result, radiation)


def solution(mesh):
    return jax.shard_map(
        body,
        mesh=mesh,
        in_specs=(
            P(None, ("ta", "pb")),
            P(("ta", "pb")),
            P(("ta", "pb")),
            P(("ta", "pb"), None),
            P(("ta", "pb")),
            P(),
            P(),
            P(),
            P(),
            P(),
            P(),
        ),
        out_specs=(P(None, ("ta", "pb")), P(None, "ta")),
        check_vma=False,
    )
```

```python
import math

import jax
import jax.numpy as jnp
from jax import lax
from jax.sharding import PartitionSpec as P

SL_DEV = 4
PS_DEV = 1024
HARM = 48
PERIODS = 2


DISPERSION = 3.0
LASER_GAIN = 1.0
KICK_GAIN = 0.5
SLIP_GAIN = 0.05


def shifted(value, axis, steps):
    count = lax.axis_size(axis)
    leading, last = (max(0, -steps), min(count, count - steps))
    return lax.ppermute(value, axis, [(source, source + steps) for source in range(leading, last)])


def lookup(values_table, positions):
    matches = (
        positions[None, :] == jnp.arange(values_table.shape[0], dtype=jnp.int32)[:, None]
    ).astype(jnp.bfloat16)
    table_parts = jnp.stack(split3(values_table))
    picked = jnp.dot(table_parts, matches, preferred_element_type=jnp.float32)
    return (picked[0] + picked[1]) + picked[2]


def split3(x):
    hi = lax.reduce_precision(x, exponent_bits=8, mantissa_bits=7)
    rest = x - hi
    mid = lax.reduce_precision(rest, exponent_bits=8, mantissa_bits=7)
    lo = rest - mid
    return [part.astype(jnp.bfloat16) for part in (hi, mid, lo)]


def arrival_slots(to_group):
    groups, count = to_group.shape
    block_size = math.gcd(count, 512)
    turn_count = count // block_size
    onehot = to_group.astype(jnp.bfloat16).reshape(groups, turn_count, block_size)
    earlier = (jnp.arange(block_size)[:, None] > jnp.arange(block_size)[None, :]).astype(
        jnp.bfloat16
    )
    within = jnp.einsum("gtj,ij->gti", onehot, earlier, preferred_element_type=jnp.float32)
    rows_f = onehot.astype(jnp.float32)
    per_turn = jnp.sum(rows_f, axis=2)
    offsets = jnp.cumsum(per_turn, axis=1) - per_turn
    arrival = jnp.sum((within + offsets[:, :, None]) * rows_f, axis=0)
    return arrival.reshape(count).astype(jnp.int32)


def deposit_rows(weight_bf16, row_key, col, targets, grid_y):
    left = jnp.where(
        row_key[None, :] == targets[:, None], weight_bf16[None, :], jnp.zeros((), jnp.bfloat16)
    )
    right = (jnp.arange(grid_y, dtype=jnp.int32)[:, None] == col[None, :]).astype(jnp.bfloat16)
    return lax.dot_general(
        left, right, (((1,), (1,)), ((), ())), preferred_element_type=jnp.float32
    )


def pb_sum(rows, axis):
    count = lax.axis_size(axis)
    chunks = rows.reshape((count, -1) + rows.shape[1:])
    mine = jnp.sum(lax.all_to_all(chunks, axis, 0, 0, tiled=True), axis=0)
    every = lax.all_to_all(jnp.broadcast_to(mine[None], chunks.shape), axis, 0, 0, tiled=True)
    return every.reshape(rows.shape)


def pb_sum_small(value, axis):
    count = lax.axis_size(axis)
    spread = jnp.broadcast_to(value[None], (count,) + value.shape)
    return jnp.sum(lax.all_to_all(spread, axis, 0, 0, tiled=True), axis=0)


def stencil(extended, coeff_long, coeff_cross):
    centre = extended[1:-1]
    along_diff = extended[2:] - extended[:-2]
    padded_x = jnp.pad(centre, ((0, 0), (1, 1), (0, 0)))
    across = padded_x[:, 2:, :] + padded_x[:, :-2, :]
    padded_y = jnp.pad(centre, ((0, 0), (0, 0), (1, 1)))
    upper_y = padded_y[:, :, 2:]
    lower_y = padded_y[:, :, :-2]
    return coeff_long[None] * along_diff + coeff_cross[None] * (
        4.0 * centre - across - upper_y - lower_y
    )


def body(
    particles,
    weights,
    cell_index,
    target_group,
    target_slice,
    laser_x,
    laser_y,
    mode_x,
    mode_y,
    along_coeff,
    across_coeff,
):
    groups = lax.axis_size("ta")
    splits = lax.axis_size("pb")
    grid_x = laser_x.shape[0]
    grid_y = laser_y.shape[0]
    cell_count = grid_x * grid_y
    per_device = particles.shape[1]
    capacity = 2 * per_device // groups
    slot_count = groups * capacity
    row_x = cell_index // grid_y
    row_y = cell_index % grid_y
    energy = particles[1] + LASER_GAIN * lookup(laser_x, row_x) * lookup(laser_y, row_y) * jnp.sin(
        particles[0]
    )
    phases = particles[0] + DISPERSION * energy
    destination = target_group.reshape(1, per_device)
    to_group = lax.optimization_barrier(destination == jnp.arange(groups, dtype=jnp.int32)[:, None])
    arrival = arrival_slots(to_group)

    values = jnp.stack(
        [
            phases,
            energy,
            weights.astype(jnp.float32),
            (target_slice * cell_count + cell_index).astype(jnp.float32),
        ]
    )
    value_count = values.shape[0]
    parts = split3(values)
    left = jnp.concatenate(
        [
            jnp.where(to_group[None], part[:, None, :], jnp.zeros((), jnp.bfloat16)).reshape(
                value_count * groups, per_device
            )
            for part in parts
        ]
    )
    to_slot = (arrival[:, None] == jnp.arange(capacity, dtype=jnp.int32)[None, :]).astype(
        jnp.bfloat16
    )
    placed = jnp.dot(left, to_slot, preferred_element_type=jnp.float32)
    rows = value_count * groups
    send = (placed[:rows] + placed[rows : 2 * rows]) + placed[2 * rows :]
    got = lax.all_to_all(
        send.reshape(value_count, groups, capacity), "ta", split_axis=1, concat_axis=1, tiled=True
    ).reshape(value_count, slot_count)

    got_phase = got[0]
    got_energy = got[1]
    arrived_weight = got[2]
    combined = got[3].astype(jnp.int32)
    got_slice = combined // cell_count
    got_cell = combined % cell_count
    got_x = got_cell // grid_y
    got_y = got_cell % grid_y
    row_key = got_slice * grid_x + got_x
    weight_bf16 = arrived_weight.astype(jnp.bfloat16)

    density_rows = SL_DEV * grid_x
    partial = deposit_rows(
        weight_bf16, row_key, got_y, jnp.arange(density_rows, dtype=jnp.int32), grid_y
    )

    profile = lookup(mode_x, got_x) * lookup(mode_y, got_y)
    weighted = arrived_weight * profile
    select = (got_slice[None, :] == jnp.arange(SL_DEV, dtype=jnp.int32)[:, None]).astype(
        jnp.float32
    )

    def local_bunching(phase):
        harmonic_phase = HARM * phase
        cosine = jnp.cos(harmonic_phase)
        sine_part = jnp.sin(harmonic_phase)
        sums = jnp.stack(
            [
                jnp.sum(select * (weighted * cosine)[None, :], axis=1),
                jnp.sum(select * (-weighted * sine_part)[None, :], axis=1),
            ]
        )
        return cosine, sine_part, sums

    cosine0, sine0, sums0 = local_bunching(got_phase)
    lanes = -(-(grid_y + 2 * SL_DEV) // 128) * 128
    chunk_rows = -(-density_rows // (splits * 8)) * 8
    side = jnp.pad(
        sums0.reshape(1, 2 * SL_DEV),
        ((0, chunk_rows * splits - 1), (0, lanes - grid_y - 2 * SL_DEV)),
    )
    stacked = jnp.pad(partial, ((0, chunk_rows * splits - density_rows), (0, 0)))
    stacked = jnp.concatenate([stacked, side], axis=1)
    summed = pb_sum(stacked, "pb")
    density = summed[:density_rows, :grid_y].reshape(SL_DEV, grid_x, grid_y)
    bunching0 = summed[0, grid_y : grid_y + 2 * SL_DEV].reshape(2, SL_DEV)

    couple = 1.0 / math.sqrt(splits * PS_DEV)
    radiation0 = couple * bunching0
    last_row = jnp.pad(radiation0[:, -1:].reshape(1, 2), ((0, 7), (0, grid_y - 2)))
    halo_below = shifted(jnp.concatenate([density[SL_DEV - 1], last_row]), "ta", 1)
    above = shifted(density[0], "ta", -1)
    empty = jnp.zeros((1, grid_x, grid_y), jnp.float32)
    force_map = stencil(jnp.concatenate([empty, density, empty]), along_coeff, across_coeff)

    def pick(table, key, key_count):
        table_hi = lax.reduce_precision(table, exponent_bits=8, mantissa_bits=7)
        table_parts = jnp.concatenate(
            [table_hi.astype(jnp.bfloat16), (table - table_hi).astype(jnp.bfloat16)], axis=1
        ).T
        pick_row = (jnp.arange(key_count, dtype=jnp.int32)[:, None] == key[None, :]).astype(
            jnp.bfloat16
        )
        picked = jnp.dot(table_parts, pick_row, preferred_element_type=jnp.float32)
        picked = picked[:grid_y] + picked[grid_y:]
        return jnp.sum(jnp.where(pick_col, picked, 0.0), axis=0)

    pick_col = jnp.arange(grid_y, dtype=jnp.int32)[:, None] == got_y[None, :]
    force_here = pick(force_map.reshape(SL_DEV * grid_x, grid_y), row_key, SL_DEV * grid_x)
    below_density = halo_below[:grid_x]
    halo_force = jnp.concatenate([-along_coeff * below_density, along_coeff * above]).reshape(
        2 * grid_x, grid_y
    )
    halo_key = jnp.where(
        got_slice == 0, got_x, jnp.where(got_slice == SL_DEV - 1, got_x + grid_x, -1)
    )
    halo_here = pick(halo_force, halo_key, 2 * grid_x)
    kicked = got_energy + (force_here + halo_here)

    radiation = jnp.zeros((2, SL_DEV), jnp.float32)
    for period in range(PERIODS):
        if period == 0:
            cosine, sine_part = cosine0, sine0
            radiation = radiation + radiation0
        else:
            cosine, sine_part, local_sums = local_bunching(got_phase)
            bunching = pb_sum_small(local_sums, "pb")
            radiation = radiation + couple * bunching
        real_here = jnp.sum(select * radiation[0][:, None], axis=0)
        imag_here = jnp.sum(select * radiation[1][:, None], axis=0)
        kicked = kicked + KICK_GAIN * profile * (real_here * cosine - imag_here * sine_part)
        got_phase = got_phase + SLIP_GAIN * kicked
        if period == 0:
            incoming = halo_below[grid_x, :2].reshape(2, 1)
        else:
            incoming = shifted(radiation[:, -1:], "ta", 1)
        radiation = jnp.concatenate([incoming, radiation[:, :-1]], axis=1)
    filled = arrived_weight > 0
    result = jnp.stack([jnp.where(filled, got_phase, 0.0), jnp.where(filled, kicked, 0.0)])
    return (result, radiation)


def solution(mesh):
    return jax.shard_map(
        body,
        mesh=mesh,
        in_specs=(
            P(None, ("ta", "pb")),
            P(("ta", "pb")),
            P(("ta", "pb")),
            P(("ta", "pb"), None),
            P(("ta", "pb")),
            P(),
            P(),
            P(),
            P(),
            P(),
            P(),
        ),
        out_specs=(P(None, ("ta", "pb")), P(None, "ta")),
        check_vma=False,
    )
```

```python
import math

import jax
import jax.numpy as jnp
from jax import lax
from jax.sharding import PartitionSpec as P

SL_DEV = 4
PS_DEV = 1024
HARM = 48
PERIODS = 2


DISPERSION = 3.0
LASER_GAIN = 1.0
KICK_GAIN = 0.5
SLIP_GAIN = 0.05


def shifted(value, axis, steps):
    count = lax.axis_size(axis)
    leading, last = (max(0, -steps), min(count, count - steps))
    return lax.ppermute(value, axis, [(source, source + steps) for source in range(leading, last)])


def lookup(values_table, positions):
    matches = positions[None, :] == jnp.arange(values_table.shape[0], dtype=jnp.int32)[:, None]
    return jnp.sum(jnp.where(matches, values_table[:, None], 0.0), axis=0)


def split3(x):
    hi = lax.reduce_precision(x, exponent_bits=8, mantissa_bits=7)
    rest = x - hi
    mid = lax.reduce_precision(rest, exponent_bits=8, mantissa_bits=7)
    lo = rest - mid
    return [part.astype(jnp.bfloat16) for part in (hi, mid, lo)]


def arrival_slots(to_group):
    groups, count = to_group.shape
    block_size = math.gcd(count, 512)
    turn_count = count // block_size
    onehot = to_group.astype(jnp.bfloat16).reshape(groups, turn_count, block_size)
    earlier = (jnp.arange(block_size)[:, None] > jnp.arange(block_size)[None, :]).astype(
        jnp.bfloat16
    )
    within = jnp.einsum("gtj,ij->gti", onehot, earlier, preferred_element_type=jnp.float32)
    rows_f = onehot.astype(jnp.float32)
    per_turn = jnp.sum(rows_f, axis=2)
    offsets = jnp.cumsum(per_turn, axis=1) - per_turn
    arrival = jnp.sum((within + offsets[:, :, None]) * rows_f, axis=0)
    return arrival.reshape(count).astype(jnp.int32)


def deposit_rows(weight_bf16, row_key, col, targets, grid_y):
    left = jnp.where(
        row_key[None, :] == targets[:, None], weight_bf16[None, :], jnp.zeros((), jnp.bfloat16)
    )
    right = (jnp.arange(grid_y, dtype=jnp.int32)[:, None] == col[None, :]).astype(jnp.bfloat16)
    return lax.dot_general(
        left, right, (((1,), (1,)), ((), ())), preferred_element_type=jnp.float32
    )


def pb_sum(rows, axis):
    count = lax.axis_size(axis)
    chunks = rows.reshape((count, -1) + rows.shape[1:])
    mine = jnp.sum(lax.all_to_all(chunks, axis, 0, 0, tiled=True), axis=0)
    every = lax.all_to_all(jnp.broadcast_to(mine[None], chunks.shape), axis, 0, 0, tiled=True)
    return every.reshape(rows.shape)


def pb_sum_small(value, axis):
    count = lax.axis_size(axis)
    spread = jnp.broadcast_to(value[None], (count,) + value.shape)
    return jnp.sum(lax.all_to_all(spread, axis, 0, 0, tiled=True), axis=0)


def stencil(extended, coeff_long, coeff_cross):
    centre = extended[1:-1]
    along_diff = extended[2:] - extended[:-2]
    padded_x = jnp.pad(centre, ((0, 0), (1, 1), (0, 0)))
    across = padded_x[:, 2:, :] + padded_x[:, :-2, :]
    padded_y = jnp.pad(centre, ((0, 0), (0, 0), (1, 1)))
    upper_y = padded_y[:, :, 2:]
    lower_y = padded_y[:, :, :-2]
    return coeff_long[None] * along_diff + coeff_cross[None] * (
        4.0 * centre - across - upper_y - lower_y
    )


def body(
    particles,
    weights,
    cell_index,
    target_group,
    target_slice,
    laser_x,
    laser_y,
    mode_x,
    mode_y,
    along_coeff,
    across_coeff,
):
    groups = lax.axis_size("ta")
    splits = lax.axis_size("pb")
    grid_x = laser_x.shape[0]
    grid_y = laser_y.shape[0]
    cell_count = grid_x * grid_y
    per_device = particles.shape[1]
    capacity = 2 * per_device // groups
    slot_count = groups * capacity
    row_x = cell_index // grid_y
    row_y = cell_index % grid_y
    energy = particles[1] + LASER_GAIN * lookup(laser_x, row_x) * lookup(laser_y, row_y) * jnp.sin(
        particles[0]
    )
    phases = particles[0] + DISPERSION * energy
    destination = target_group.reshape(1, per_device)
    to_group = lax.optimization_barrier(destination == jnp.arange(groups, dtype=jnp.int32)[:, None])
    arrival = arrival_slots(to_group)

    values = jnp.stack(
        [
            phases,
            energy,
            weights.astype(jnp.float32),
            (target_slice * cell_count + cell_index).astype(jnp.float32),
        ]
    )
    value_count = values.shape[0]
    parts = split3(values)
    left = jnp.concatenate(
        [
            jnp.where(to_group[None], part[:, None, :], jnp.zeros((), jnp.bfloat16)).reshape(
                value_count * groups, per_device
            )
            for part in parts
        ]
    )
    to_slot = (arrival[:, None] == jnp.arange(capacity, dtype=jnp.int32)[None, :]).astype(
        jnp.bfloat16
    )
    placed = jnp.dot(left, to_slot, preferred_element_type=jnp.float32)
    rows = value_count * groups
    send = (placed[:rows] + placed[rows : 2 * rows]) + placed[2 * rows :]
    got = lax.all_to_all(
        send.reshape(value_count, groups, capacity), "ta", split_axis=1, concat_axis=1, tiled=True
    ).reshape(value_count, slot_count)

    got_phase = got[0]
    got_energy = got[1]
    arrived_weight = got[2]
    combined = got[3].astype(jnp.int32)
    got_slice = combined // cell_count
    got_cell = combined % cell_count
    got_x = got_cell // grid_y
    got_y = got_cell % grid_y
    row_key = got_slice * grid_x + got_x
    weight_bf16 = arrived_weight.astype(jnp.bfloat16)

    density_rows = SL_DEV * grid_x
    partial = deposit_rows(
        weight_bf16, row_key, got_y, jnp.arange(density_rows, dtype=jnp.int32), grid_y
    )

    profile = lookup(mode_x, got_x) * lookup(mode_y, got_y)
    weighted = arrived_weight * profile
    select = (got_slice[None, :] == jnp.arange(SL_DEV, dtype=jnp.int32)[:, None]).astype(
        jnp.float32
    )

    def local_bunching(phase):
        harmonic_phase = HARM * phase
        cosine = jnp.cos(harmonic_phase)
        sine_part = jnp.sin(harmonic_phase)
        sums = jnp.stack(
            [
                jnp.sum(select * (weighted * cosine)[None, :], axis=1),
                jnp.sum(select * (-weighted * sine_part)[None, :], axis=1),
            ]
        )
        return cosine, sine_part, sums

    cosine0, sine0, sums0 = local_bunching(got_phase)
    lanes = -(-(grid_y + 2 * SL_DEV) // 128) * 128
    chunk_rows = -(-density_rows // (splits * 8)) * 8
    side = jnp.pad(
        sums0.reshape(1, 2 * SL_DEV),
        ((0, chunk_rows * splits - 1), (0, lanes - grid_y - 2 * SL_DEV)),
    )
    stacked = jnp.pad(partial, ((0, chunk_rows * splits - density_rows), (0, 0)))
    stacked = jnp.concatenate([stacked, side], axis=1)
    summed = pb_sum(stacked, "pb")
    density = summed[:density_rows, :grid_y].reshape(SL_DEV, grid_x, grid_y)
    bunching0 = summed[0, grid_y : grid_y + 2 * SL_DEV].reshape(2, SL_DEV)

    couple = 1.0 / math.sqrt(splits * PS_DEV)
    radiation0 = couple * bunching0
    last_row = jnp.pad(radiation0[:, -1:].reshape(1, 2), ((0, 7), (0, grid_y - 2)))
    halo_below = shifted(jnp.concatenate([density[SL_DEV - 1], last_row]), "ta", 1)
    above = shifted(density[0], "ta", -1)
    empty = jnp.zeros((1, grid_x, grid_y), jnp.float32)
    force_map = stencil(jnp.concatenate([empty, density, empty]), along_coeff, across_coeff)

    def pick(table, key, key_count):
        table_hi = lax.reduce_precision(table, exponent_bits=8, mantissa_bits=7)
        table_parts = jnp.concatenate(
            [table_hi.astype(jnp.bfloat16), (table - table_hi).astype(jnp.bfloat16)], axis=1
        ).T
        pick_row = (jnp.arange(key_count, dtype=jnp.int32)[:, None] == key[None, :]).astype(
            jnp.bfloat16
        )
        picked = jnp.dot(table_parts, pick_row, preferred_element_type=jnp.float32)
        picked = picked[:grid_y] + picked[grid_y:]
        return jnp.sum(jnp.where(pick_col, picked, 0.0), axis=0)

    pick_col = jnp.arange(grid_y, dtype=jnp.int32)[:, None] == got_y[None, :]
    force_here = pick(force_map.reshape(SL_DEV * grid_x, grid_y), row_key, SL_DEV * grid_x)
    below_density = halo_below[:grid_x]
    halo_force = jnp.concatenate([-along_coeff * below_density, along_coeff * above]).reshape(
        2 * grid_x, grid_y
    )
    halo_key = jnp.where(
        got_slice == 0, got_x, jnp.where(got_slice == SL_DEV - 1, got_x + grid_x, -1)
    )
    halo_here = pick(halo_force, halo_key, 2 * grid_x)
    kicked = got_energy + (force_here + halo_here)

    radiation = jnp.zeros((2, SL_DEV), jnp.float32)
    for period in range(PERIODS):
        if period == 0:
            cosine, sine_part = cosine0, sine0
            radiation = radiation + radiation0
        else:
            cosine, sine_part, local_sums = local_bunching(got_phase)
            cosine, sine_part = lax.optimization_barrier((cosine, sine_part))
            bunching = pb_sum_small(local_sums, "pb")
            radiation = radiation + couple * bunching
        real_here = jnp.sum(select * radiation[0][:, None], axis=0)
        imag_here = jnp.sum(select * radiation[1][:, None], axis=0)
        kicked = kicked + KICK_GAIN * profile * (real_here * cosine - imag_here * sine_part)
        got_phase = got_phase + SLIP_GAIN * kicked
        if period == 0:
            incoming = halo_below[grid_x, :2].reshape(2, 1)
        else:
            incoming = shifted(radiation[:, -1:], "ta", 1)
        radiation = jnp.concatenate([incoming, radiation[:, :-1]], axis=1)
    filled = arrived_weight > 0
    result = jnp.stack([jnp.where(filled, got_phase, 0.0), jnp.where(filled, kicked, 0.0)])
    return (result, radiation)


def solution(mesh):
    return jax.shard_map(
        body,
        mesh=mesh,
        in_specs=(
            P(None, ("ta", "pb")),
            P(("ta", "pb")),
            P(("ta", "pb")),
            P(("ta", "pb"), None),
            P(("ta", "pb")),
            P(),
            P(),
            P(),
            P(),
            P(),
            P(),
        ),
        out_specs=(P(None, ("ta", "pb")), P(None, "ta")),
        check_vma=False,
    )
```

```python
import math

import jax
import jax.numpy as jnp
from jax import lax
from jax.sharding import PartitionSpec as P

SL_DEV = 4
PS_DEV = 1024
HARM = 48
PERIODS = 2


DISPERSION = 3.0
LASER_GAIN = 1.0
KICK_GAIN = 0.5
SLIP_GAIN = 0.05


def shifted(value, axis, steps):
    count = lax.axis_size(axis)
    leading, last = (max(0, -steps), min(count, count - steps))
    return lax.ppermute(value, axis, [(source, source + steps) for source in range(leading, last)])


def lookup(values_table, positions):
    matches = positions[None, :] == jnp.arange(values_table.shape[0], dtype=jnp.int32)[:, None]
    return jnp.sum(jnp.where(matches, values_table[:, None], 0.0), axis=0)


def split3(x):
    hi = lax.reduce_precision(x, exponent_bits=8, mantissa_bits=7)
    rest = x - hi
    mid = lax.reduce_precision(rest, exponent_bits=8, mantissa_bits=7)
    lo = rest - mid
    return [part.astype(jnp.bfloat16) for part in (hi, mid, lo)]


def arrival_slots(to_group):
    groups, count = to_group.shape
    block_size = math.gcd(count, 512)
    turn_count = count // block_size
    onehot = to_group.astype(jnp.bfloat16).reshape(groups, turn_count, block_size)
    earlier = (jnp.arange(block_size)[:, None] > jnp.arange(block_size)[None, :]).astype(
        jnp.bfloat16
    )
    within = jnp.einsum("gtj,ij->gti", onehot, earlier, preferred_element_type=jnp.float32)
    rows_f = onehot.astype(jnp.float32)
    per_turn = jnp.sum(rows_f, axis=2)
    offsets = jnp.cumsum(per_turn, axis=1) - per_turn
    arrival = jnp.sum((within + offsets[:, :, None]) * rows_f, axis=0)
    return arrival.reshape(count).astype(jnp.int32)


def deposit_rows(weight_bf16, row_key, col, targets, grid_y):
    left = jnp.where(
        row_key[None, :] == targets[:, None], weight_bf16[None, :], jnp.zeros((), jnp.bfloat16)
    )
    right = (jnp.arange(grid_y, dtype=jnp.int32)[:, None] == col[None, :]).astype(jnp.bfloat16)
    return lax.dot_general(
        left, right, (((1,), (1,)), ((), ())), preferred_element_type=jnp.float32
    )


def pb_sum(rows, axis):
    count = lax.axis_size(axis)
    chunks = rows.reshape((count, -1) + rows.shape[1:])
    mine = jnp.sum(lax.all_to_all(chunks, axis, 0, 0, tiled=True), axis=0)
    every = lax.all_to_all(jnp.broadcast_to(mine[None], chunks.shape), axis, 0, 0, tiled=True)
    return every.reshape(rows.shape)


def pb_sum_small(value, axis):
    count = lax.axis_size(axis)
    spread = jnp.broadcast_to(value[None], (count,) + value.shape)
    return jnp.sum(lax.all_to_all(spread, axis, 0, 0, tiled=True), axis=0)


def stencil(extended, coeff_long, coeff_cross):
    centre = extended[1:-1]
    along_diff = extended[2:] - extended[:-2]
    padded_x = jnp.pad(centre, ((0, 0), (1, 1), (0, 0)))
    across = padded_x[:, 2:, :] + padded_x[:, :-2, :]
    padded_y = jnp.pad(centre, ((0, 0), (0, 0), (1, 1)))
    upper_y = padded_y[:, :, 2:]
    lower_y = padded_y[:, :, :-2]
    return coeff_long[None] * along_diff + coeff_cross[None] * (
        4.0 * centre - across - upper_y - lower_y
    )


def body(
    particles,
    weights,
    cell_index,
    target_group,
    target_slice,
    laser_x,
    laser_y,
    mode_x,
    mode_y,
    along_coeff,
    across_coeff,
):
    groups = lax.axis_size("ta")
    splits = lax.axis_size("pb")
    grid_x = laser_x.shape[0]
    grid_y = laser_y.shape[0]
    cell_count = grid_x * grid_y
    per_device = particles.shape[1]
    capacity = 2 * per_device // groups
    slot_count = groups * capacity
    row_x = cell_index // grid_y
    row_y = cell_index % grid_y
    energy = particles[1] + LASER_GAIN * lookup(laser_x, row_x) * lookup(laser_y, row_y) * jnp.sin(
        particles[0]
    )
    phases = particles[0] + DISPERSION * energy
    destination = target_group.reshape(1, per_device)
    to_group = lax.optimization_barrier(destination == jnp.arange(groups, dtype=jnp.int32)[:, None])
    arrival = arrival_slots(to_group)

    values = jnp.stack(
        [
            phases,
            energy,
            weights.astype(jnp.float32),
            (target_slice * cell_count + cell_index).astype(jnp.float32),
        ]
    )
    value_count = values.shape[0]
    parts = split3(values)
    left = jnp.concatenate(
        [
            jnp.where(to_group[None], part[:, None, :], jnp.zeros((), jnp.bfloat16)).reshape(
                value_count * groups, per_device
            )
            for part in parts
        ]
    )
    to_slot = (arrival[:, None] == jnp.arange(capacity, dtype=jnp.int32)[None, :]).astype(
        jnp.bfloat16
    )
    placed = jnp.dot(left, to_slot, preferred_element_type=jnp.float32)
    rows = value_count * groups
    send = (placed[:rows] + placed[rows : 2 * rows]) + placed[2 * rows :]
    got = lax.all_to_all(
        send.reshape(value_count, groups, capacity), "ta", split_axis=1, concat_axis=1, tiled=True
    ).reshape(value_count, slot_count)

    got_phase = got[0]
    got_energy = got[1]
    arrived_weight = got[2]
    combined = got[3].astype(jnp.int32)
    got_slice = combined // cell_count
    got_cell = combined % cell_count
    got_x = got_cell // grid_y
    got_y = got_cell % grid_y
    row_key = got_slice * grid_x + got_x
    weight_bf16 = arrived_weight.astype(jnp.bfloat16)

    density_rows = SL_DEV * grid_x
    partial = deposit_rows(
        weight_bf16, row_key, got_y, jnp.arange(density_rows, dtype=jnp.int32), grid_y
    )

    profile = lookup(mode_x, got_x) * lookup(mode_y, got_y)
    weighted = arrived_weight * profile
    select = (got_slice[None, :] == jnp.arange(SL_DEV, dtype=jnp.int32)[:, None]).astype(
        jnp.float32
    )

    def local_bunching(phase):
        harmonic_phase = HARM * phase
        cosine = jnp.cos(harmonic_phase)
        sine_part = jnp.sin(harmonic_phase)
        sums = jnp.stack(
            [
                jnp.sum(select * (weighted * cosine)[None, :], axis=1),
                jnp.sum(select * (-weighted * sine_part)[None, :], axis=1),
            ]
        )
        return cosine, sine_part, sums

    cosine0, sine0, sums0 = local_bunching(got_phase)
    lanes = -(-(grid_y + 2 * SL_DEV) // 128) * 128
    chunk_rows = -(-density_rows // (splits * 8)) * 8
    side = jnp.pad(
        sums0.reshape(1, 2 * SL_DEV),
        ((0, chunk_rows * splits - 1), (0, lanes - grid_y - 2 * SL_DEV)),
    )
    stacked = jnp.pad(partial, ((0, chunk_rows * splits - density_rows), (0, 0)))
    stacked = jnp.concatenate([stacked, side], axis=1)
    summed = pb_sum(stacked, "pb")
    density = summed[:density_rows, :grid_y].reshape(SL_DEV, grid_x, grid_y)
    bunching0 = summed[0, grid_y : grid_y + 2 * SL_DEV].reshape(2, SL_DEV)

    couple = 1.0 / math.sqrt(splits * PS_DEV)
    radiation0 = couple * bunching0
    last_lanes = jnp.pad(radiation0[:, -1:].reshape(1, 2), ((0, grid_x - 1), (0, lanes - grid_y - 2)))
    halo_below = shifted(jnp.concatenate([density[SL_DEV - 1], last_lanes], axis=1), "ta", 1)
    above = shifted(density[0], "ta", -1)
    empty = jnp.zeros((1, grid_x, grid_y), jnp.float32)
    force_map = stencil(jnp.concatenate([empty, density, empty]), along_coeff, across_coeff)

    def pick(table, key, key_count):
        table_hi = lax.reduce_precision(table, exponent_bits=8, mantissa_bits=7)
        table_parts = jnp.concatenate(
            [table_hi.astype(jnp.bfloat16), (table - table_hi).astype(jnp.bfloat16)], axis=1
        ).T
        pick_row = (jnp.arange(key_count, dtype=jnp.int32)[:, None] == key[None, :]).astype(
            jnp.bfloat16
        )
        picked = jnp.dot(table_parts, pick_row, preferred_element_type=jnp.float32)
        picked = picked[:grid_y] + picked[grid_y:]
        return jnp.sum(jnp.where(pick_col, picked, 0.0), axis=0)

    pick_col = jnp.arange(grid_y, dtype=jnp.int32)[:, None] == got_y[None, :]
    force_here = pick(force_map.reshape(SL_DEV * grid_x, grid_y), row_key, SL_DEV * grid_x)
    below_density = halo_below[:, :grid_y]
    halo_force = jnp.concatenate([-along_coeff * below_density, along_coeff * above]).reshape(
        2 * grid_x, grid_y
    )
    halo_key = jnp.where(
        got_slice == 0, got_x, jnp.where(got_slice == SL_DEV - 1, got_x + grid_x, -1)
    )
    halo_here = pick(halo_force, halo_key, 2 * grid_x)
    kicked = got_energy + (force_here + halo_here)

    radiation = jnp.zeros((2, SL_DEV), jnp.float32)
    for period in range(PERIODS):
        if period == 0:
            cosine, sine_part = cosine0, sine0
            radiation = radiation + radiation0
        else:
            cosine, sine_part, local_sums = local_bunching(got_phase)
            cosine, sine_part = lax.optimization_barrier((cosine, sine_part))
            bunching = pb_sum_small(local_sums, "pb")
            radiation = radiation + couple * bunching
        real_here = jnp.sum(select * radiation[0][:, None], axis=0)
        imag_here = jnp.sum(select * radiation[1][:, None], axis=0)
        kicked = kicked + KICK_GAIN * profile * (real_here * cosine - imag_here * sine_part)
        got_phase = got_phase + SLIP_GAIN * kicked
        if period == 0:
            incoming = halo_below[0, grid_y : grid_y + 2].reshape(2, 1)
        else:
            incoming = shifted(radiation[:, -1:], "ta", 1)
        radiation = jnp.concatenate([incoming, radiation[:, :-1]], axis=1)
    filled = arrived_weight > 0
    result = jnp.stack([jnp.where(filled, got_phase, 0.0), jnp.where(filled, kicked, 0.0)])
    return (result, radiation)


def solution(mesh):
    return jax.shard_map(
        body,
        mesh=mesh,
        in_specs=(
            P(None, ("ta", "pb")),
            P(("ta", "pb")),
            P(("ta", "pb")),
            P(("ta", "pb"), None),
            P(("ta", "pb")),
            P(),
            P(),
            P(),
            P(),
            P(),
            P(),
        ),
        out_specs=(P(None, ("ta", "pb")), P(None, "ta")),
        check_vma=False,
    )
```

```python
import math

import jax
import jax.numpy as jnp
from jax import lax
from jax.sharding import PartitionSpec as P

SL_DEV = 4
PS_DEV = 1024
HARM = 48
PERIODS = 2


DISPERSION = 3.0
LASER_GAIN = 1.0
KICK_GAIN = 0.5
SLIP_GAIN = 0.05


def shifted(value, axis, steps):
    count = lax.axis_size(axis)
    leading, last = (max(0, -steps), min(count, count - steps))
    return lax.ppermute(value, axis, [(source, source + steps) for source in range(leading, last)])


def lookup(values_table, positions):
    matches = positions[None, :] == jnp.arange(values_table.shape[0], dtype=jnp.int32)[:, None]
    return jnp.sum(jnp.where(matches, values_table[:, None], 0.0), axis=0)


def split3(x):
    hi = lax.reduce_precision(x, exponent_bits=8, mantissa_bits=7)
    rest = x - hi
    mid = lax.reduce_precision(rest, exponent_bits=8, mantissa_bits=7)
    lo = rest - mid
    return [part.astype(jnp.bfloat16) for part in (hi, mid, lo)]


def arrival_slots(to_group):
    groups, count = to_group.shape
    block_size = math.gcd(count, 512)
    turn_count = count // block_size
    onehot = to_group.astype(jnp.bfloat16).reshape(groups, turn_count, block_size)
    earlier = (jnp.arange(block_size)[:, None] > jnp.arange(block_size)[None, :]).astype(
        jnp.bfloat16
    )
    within = jnp.einsum("gtj,ij->gti", onehot, earlier, preferred_element_type=jnp.float32)
    rows_f = onehot.astype(jnp.float32)
    per_turn = jnp.sum(rows_f, axis=2)
    offsets = jnp.cumsum(per_turn, axis=1) - per_turn
    arrival = jnp.sum((within + offsets[:, :, None]) * rows_f, axis=0)
    return arrival.reshape(count).astype(jnp.int32)


def deposit_rows(weight_bf16, row_key, col, targets, grid_y):
    left = jnp.where(
        row_key[None, :] == targets[:, None], weight_bf16[None, :], jnp.zeros((), jnp.bfloat16)
    )
    right = (jnp.arange(grid_y, dtype=jnp.int32)[:, None] == col[None, :]).astype(jnp.bfloat16)
    return lax.dot_general(
        left, right, (((1,), (1,)), ((), ())), preferred_element_type=jnp.float32
    )


def pb_sum(rows, axis):
    count = lax.axis_size(axis)
    chunks = rows.reshape((count, -1) + rows.shape[1:])
    mine = jnp.sum(lax.all_to_all(chunks, axis, 0, 0, tiled=True), axis=0)
    every = lax.all_to_all(jnp.broadcast_to(mine[None], chunks.shape), axis, 0, 0, tiled=True)
    return every.reshape(rows.shape)


def pb_sum_small(value, axis):
    count = lax.axis_size(axis)
    spread = jnp.broadcast_to(value[None], (count,) + value.shape)
    return jnp.sum(lax.all_to_all(spread, axis, 0, 0, tiled=True), axis=0)


def stencil(extended, coeff_long, coeff_cross):
    centre = extended[1:-1]
    along_diff = extended[2:] - extended[:-2]
    padded_x = jnp.pad(centre, ((0, 0), (1, 1), (0, 0)))
    across = padded_x[:, 2:, :] + padded_x[:, :-2, :]
    padded_y = jnp.pad(centre, ((0, 0), (0, 0), (1, 1)))
    upper_y = padded_y[:, :, 2:]
    lower_y = padded_y[:, :, :-2]
    return coeff_long[None] * along_diff + coeff_cross[None] * (
        4.0 * centre - across - upper_y - lower_y
    )


def body(
    particles,
    weights,
    cell_index,
    target_group,
    target_slice,
    laser_x,
    laser_y,
    mode_x,
    mode_y,
    along_coeff,
    across_coeff,
):
    groups = lax.axis_size("ta")
    splits = lax.axis_size("pb")
    grid_x = laser_x.shape[0]
    grid_y = laser_y.shape[0]
    cell_count = grid_x * grid_y
    per_device = particles.shape[1]
    capacity = 2 * per_device // groups
    slot_count = groups * capacity
    row_x = cell_index // grid_y
    row_y = cell_index % grid_y
    energy = particles[1] + LASER_GAIN * lookup(laser_x, row_x) * lookup(laser_y, row_y) * jnp.sin(
        particles[0]
    )
    phases = particles[0] + DISPERSION * energy
    destination = target_group.reshape(1, per_device)
    to_group = lax.optimization_barrier(destination == jnp.arange(groups, dtype=jnp.int32)[:, None])
    arrival = arrival_slots(to_group)

    values = jnp.stack(
        [
            phases,
            energy,
            weights.astype(jnp.float32),
            (target_slice * cell_count + cell_index).astype(jnp.float32),
        ]
    )
    value_count = values.shape[0]
    parts = split3(values)
    left = jnp.concatenate(
        [
            jnp.where(to_group[None], part[:, None, :], jnp.zeros((), jnp.bfloat16)).reshape(
                value_count * groups, per_device
            )
            for part in parts
        ]
    )
    to_slot = (arrival[:, None] == jnp.arange(capacity, dtype=jnp.int32)[None, :]).astype(
        jnp.bfloat16
    )
    placed = jnp.dot(left, to_slot, preferred_element_type=jnp.float32)
    rows = value_count * groups
    send = (placed[:rows] + placed[rows : 2 * rows]) + placed[2 * rows :]
    got = lax.all_to_all(
        send.reshape(value_count, groups, capacity), "ta", split_axis=1, concat_axis=1, tiled=True
    ).reshape(value_count, slot_count)

    got_phase = got[0]
    got_energy = got[1]
    arrived_weight = got[2]
    combined = got[3].astype(jnp.int32)
    got_slice = combined // cell_count
    got_cell = combined % cell_count
    got_x = got_cell // grid_y
    got_y = got_cell % grid_y
    row_key = got_slice * grid_x + got_x
    weight_bf16 = arrived_weight.astype(jnp.bfloat16)

    density_rows = SL_DEV * grid_x
    partial = deposit_rows(
        weight_bf16, row_key, got_y, jnp.arange(density_rows, dtype=jnp.int32), grid_y
    )

    profile = lookup(mode_x, got_x) * lookup(mode_y, got_y)
    weighted = arrived_weight * profile
    select = (got_slice[None, :] == jnp.arange(SL_DEV, dtype=jnp.int32)[:, None]).astype(
        jnp.float32
    )

    def local_bunching(phase):
        harmonic_phase = HARM * phase
        cosine = jnp.cos(harmonic_phase)
        sine_part = jnp.sin(harmonic_phase)
        sums = jnp.stack(
            [
                jnp.sum(select * (weighted * cosine)[None, :], axis=1),
                jnp.sum(select * (-weighted * sine_part)[None, :], axis=1),
            ]
        )
        return cosine, sine_part, sums

    cosine0, sine0, sums0 = local_bunching(got_phase)
    lanes = -(-(grid_y + 2 * SL_DEV) // 128) * 128
    chunk_rows = -(-density_rows // (splits * 8)) * 8
    side = jnp.pad(
        sums0.reshape(1, 2 * SL_DEV),
        ((0, chunk_rows * splits - 1), (0, lanes - grid_y - 2 * SL_DEV)),
    )
    stacked = jnp.pad(partial, ((0, chunk_rows * splits - density_rows), (0, 0)))
    stacked = jnp.concatenate([stacked, side], axis=1)
    summed = pb_sum(stacked, "pb")
    density = summed[:density_rows, :grid_y].reshape(SL_DEV, grid_x, grid_y)
    bunching0 = summed[0, grid_y : grid_y + 2 * SL_DEV].reshape(2, SL_DEV)

    couple = 1.0 / math.sqrt(splits * PS_DEV)
    radiation0 = couple * bunching0
    last_row = jnp.pad(radiation0[:, -1:].reshape(1, 2), ((0, 7), (0, grid_y - 2)))
    halo_below = shifted(jnp.concatenate([density[SL_DEV - 1], last_row]), "ta", 1)
    above = shifted(density[0], "ta", -1)
    empty = jnp.zeros((1, grid_x, grid_y), jnp.float32)
    force_map = stencil(jnp.concatenate([empty, density, empty]), along_coeff, across_coeff)

    def pick(table, key, key_count, early=False):
        table_hi = lax.reduce_precision(table, exponent_bits=8, mantissa_bits=7)
        table_parts = jnp.concatenate(
            [table_hi.astype(jnp.bfloat16), (table - table_hi).astype(jnp.bfloat16)], axis=1
        ).T
        pick_row = jnp.arange(key_count, dtype=jnp.int32)[:, None] == key[None, :]
        if early:
            pick_row = lax.optimization_barrier(pick_row)
        pick_row = pick_row.astype(jnp.bfloat16)
        picked = jnp.dot(table_parts, pick_row, preferred_element_type=jnp.float32)
        picked = picked[:grid_y] + picked[grid_y:]
        return jnp.sum(jnp.where(pick_col, picked, 0.0), axis=0)

    pick_col = jnp.arange(grid_y, dtype=jnp.int32)[:, None] == got_y[None, :]
    force_here = pick(force_map.reshape(SL_DEV * grid_x, grid_y), row_key, SL_DEV * grid_x)
    below_density = halo_below[:grid_x]
    halo_force = jnp.concatenate([-along_coeff * below_density, along_coeff * above]).reshape(
        2 * grid_x, grid_y
    )
    halo_key = jnp.where(
        got_slice == 0, got_x, jnp.where(got_slice == SL_DEV - 1, got_x + grid_x, -1)
    )
    halo_here = pick(halo_force, halo_key, 2 * grid_x, early=True)
    kicked = got_energy + (force_here + halo_here)

    radiation = jnp.zeros((2, SL_DEV), jnp.float32)
    for period in range(PERIODS):
        if period == 0:
            cosine, sine_part = cosine0, sine0
            radiation = radiation + radiation0
        else:
            cosine, sine_part, local_sums = local_bunching(got_phase)
            cosine, sine_part = lax.optimization_barrier((cosine, sine_part))
            bunching = pb_sum_small(local_sums, "pb")
            radiation = radiation + couple * bunching
        real_here = jnp.sum(select * radiation[0][:, None], axis=0)
        imag_here = jnp.sum(select * radiation[1][:, None], axis=0)
        kicked = kicked + KICK_GAIN * profile * (real_here * cosine - imag_here * sine_part)
        got_phase = got_phase + SLIP_GAIN * kicked
        if period == 0:
            incoming = halo_below[grid_x, :2].reshape(2, 1)
        else:
            incoming = shifted(radiation[:, -1:], "ta", 1)
        radiation = jnp.concatenate([incoming, radiation[:, :-1]], axis=1)
    filled = arrived_weight > 0
    result = jnp.stack([jnp.where(filled, got_phase, 0.0), jnp.where(filled, kicked, 0.0)])
    return (result, radiation)


def solution(mesh):
    return jax.shard_map(
        body,
        mesh=mesh,
        in_specs=(
            P(None, ("ta", "pb")),
            P(("ta", "pb")),
            P(("ta", "pb")),
            P(("ta", "pb"), None),
            P(("ta", "pb")),
            P(),
            P(),
            P(),
            P(),
            P(),
            P(),
        ),
        out_specs=(P(None, ("ta", "pb")), P(None, "ta")),
        check_vma=False,
    )
```

```python
import math

import jax
import jax.numpy as jnp
from jax import lax
from jax.sharding import PartitionSpec as P

SL_DEV = 4
PS_DEV = 1024
HARM = 48
PERIODS = 2


DISPERSION = 3.0
LASER_GAIN = 1.0
KICK_GAIN = 0.5
SLIP_GAIN = 0.05


def shifted(value, axis, steps):
    count = lax.axis_size(axis)
    leading, last = (max(0, -steps), min(count, count - steps))
    return lax.ppermute(value, axis, [(source, source + steps) for source in range(leading, last)])


def lookup(values_table, positions):
    matches = positions[None, :] == jnp.arange(values_table.shape[0], dtype=jnp.int32)[:, None]
    return jnp.sum(jnp.where(matches, values_table[:, None], 0.0), axis=0)


def split3(x):
    hi = lax.reduce_precision(x, exponent_bits=8, mantissa_bits=7)
    rest = x - hi
    mid = lax.reduce_precision(rest, exponent_bits=8, mantissa_bits=7)
    lo = rest - mid
    return [part.astype(jnp.bfloat16) for part in (hi, mid, lo)]


def arrival_slots(to_group):
    groups, count = to_group.shape
    block_size = math.gcd(count, 512)
    turn_count = count // block_size
    onehot = to_group.astype(jnp.bfloat16).reshape(groups, turn_count, block_size)
    earlier = (jnp.arange(block_size)[:, None] > jnp.arange(block_size)[None, :]).astype(
        jnp.bfloat16
    )
    within = jnp.einsum("gtj,ij->gti", onehot, earlier, preferred_element_type=jnp.float32)
    rows_f = onehot.astype(jnp.float32)
    per_turn = jnp.sum(rows_f, axis=2)
    offsets = jnp.cumsum(per_turn, axis=1) - per_turn
    arrival = jnp.sum((within + offsets[:, :, None]) * rows_f, axis=0)
    return arrival.reshape(count).astype(jnp.int32)


def deposit_rows(weight_bf16, row_key, col, targets, grid_y):
    left = jnp.where(
        row_key[None, :] == targets[:, None], weight_bf16[None, :], jnp.zeros((), jnp.bfloat16)
    )
    right = (jnp.arange(grid_y, dtype=jnp.int32)[:, None] == col[None, :]).astype(jnp.bfloat16)
    return lax.dot_general(
        left, right, (((1,), (1,)), ((), ())), preferred_element_type=jnp.float32
    )


def pb_sum(rows, axis):
    count = lax.axis_size(axis)
    chunks = rows.reshape((count, -1) + rows.shape[1:])
    mine = jnp.sum(lax.all_to_all(chunks, axis, 0, 0, tiled=True), axis=0)
    every = lax.all_to_all(jnp.broadcast_to(mine[None], chunks.shape), axis, 0, 0, tiled=True)
    return every.reshape(rows.shape)


def pb_sum_small(value, axis):
    count = lax.axis_size(axis)
    spread = jnp.broadcast_to(value[None], (count,) + value.shape)
    return jnp.sum(lax.all_to_all(spread, axis, 0, 0, tiled=True), axis=0)


def stencil(extended, coeff_long, coeff_cross):
    centre = extended[1:-1]
    along_diff = extended[2:] - extended[:-2]
    padded_x = jnp.pad(centre, ((0, 0), (1, 1), (0, 0)))
    across = padded_x[:, 2:, :] + padded_x[:, :-2, :]
    padded_y = jnp.pad(centre, ((0, 0), (0, 0), (1, 1)))
    upper_y = padded_y[:, :, 2:]
    lower_y = padded_y[:, :, :-2]
    return coeff_long[None] * along_diff + coeff_cross[None] * (
        4.0 * centre - across - upper_y - lower_y
    )


def body(
    particles,
    weights,
    cell_index,
    target_group,
    target_slice,
    laser_x,
    laser_y,
    mode_x,
    mode_y,
    along_coeff,
    across_coeff,
):
    groups = lax.axis_size("ta")
    splits = lax.axis_size("pb")
    grid_x = laser_x.shape[0]
    grid_y = laser_y.shape[0]
    cell_count = grid_x * grid_y
    per_device = particles.shape[1]
    capacity = 2 * per_device // groups
    slot_count = groups * capacity
    row_x = cell_index // grid_y
    row_y = cell_index % grid_y
    energy = particles[1] + LASER_GAIN * lookup(laser_x, row_x) * lookup(laser_y, row_y) * jnp.sin(
        particles[0]
    )
    phases = particles[0] + DISPERSION * energy
    destination = target_group.reshape(1, per_device)
    to_group = lax.optimization_barrier(destination == jnp.arange(groups, dtype=jnp.int32)[:, None])
    arrival = arrival_slots(to_group)

    values = jnp.stack(
        [phases, energy, (target_slice * cell_count + cell_index).astype(jnp.float32)]
    )
    weight_row = weights[None]
    parts = [
        jnp.concatenate([part, weight_row if k == 0 else jnp.zeros_like(weight_row)])
        for k, part in enumerate(split3(values))
    ]
    value_count = parts[0].shape[0]
    left = jnp.concatenate(
        [
            jnp.where(to_group[None], part[:, None, :], jnp.zeros((), jnp.bfloat16)).reshape(
                value_count * groups, per_device
            )
            for part in parts
        ]
    )
    to_slot = (arrival[:, None] == jnp.arange(capacity, dtype=jnp.int32)[None, :]).astype(
        jnp.bfloat16
    )
    placed = jnp.dot(left, to_slot, preferred_element_type=jnp.float32)
    rows = value_count * groups
    send = (placed[:rows] + placed[rows : 2 * rows]) + placed[2 * rows :]
    got = lax.all_to_all(
        send.reshape(value_count, groups, capacity), "ta", split_axis=1, concat_axis=1, tiled=True
    ).reshape(value_count, slot_count)

    got_phase = got[0]
    got_energy = got[1]
    arrived_weight = got[3]
    combined = got[2].astype(jnp.int32)
    got_slice = combined // cell_count
    got_cell = combined % cell_count
    got_x = got_cell // grid_y
    got_y = got_cell % grid_y
    row_key = got_slice * grid_x + got_x
    weight_bf16 = arrived_weight.astype(jnp.bfloat16)

    density_rows = SL_DEV * grid_x
    partial = deposit_rows(
        weight_bf16, row_key, got_y, jnp.arange(density_rows, dtype=jnp.int32), grid_y
    )

    profile = lookup(mode_x, got_x) * lookup(mode_y, got_y)
    weighted = arrived_weight * profile
    select = (got_slice[None, :] == jnp.arange(SL_DEV, dtype=jnp.int32)[:, None]).astype(
        jnp.float32
    )

    def local_bunching(phase):
        harmonic_phase = HARM * phase
        cosine = jnp.cos(harmonic_phase)
        sine_part = jnp.sin(harmonic_phase)
        sums = jnp.stack(
            [
                jnp.sum(select * (weighted * cosine)[None, :], axis=1),
                jnp.sum(select * (-weighted * sine_part)[None, :], axis=1),
            ]
        )
        return cosine, sine_part, sums

    cosine0, sine0, sums0 = local_bunching(got_phase)
    lanes = -(-(grid_y + 2 * SL_DEV) // 128) * 128
    chunk_rows = -(-density_rows // (splits * 8)) * 8
    side = jnp.pad(
        sums0.reshape(1, 2 * SL_DEV),
        ((0, chunk_rows * splits - 1), (0, lanes - grid_y - 2 * SL_DEV)),
    )
    stacked = jnp.pad(partial, ((0, chunk_rows * splits - density_rows), (0, 0)))
    stacked = jnp.concatenate([stacked, side], axis=1)
    summed = pb_sum(stacked, "pb")
    density = summed[:density_rows, :grid_y].reshape(SL_DEV, grid_x, grid_y)
    bunching0 = summed[0, grid_y : grid_y + 2 * SL_DEV].reshape(2, SL_DEV)

    couple = 1.0 / math.sqrt(splits * PS_DEV)
    radiation0 = couple * bunching0
    last_row = jnp.pad(radiation0[:, -1:].reshape(1, 2), ((0, 7), (0, grid_y - 2)))
    halo_below = shifted(jnp.concatenate([density[SL_DEV - 1], last_row]), "ta", 1)
    above = shifted(density[0], "ta", -1)
    empty = jnp.zeros((1, grid_x, grid_y), jnp.float32)
    force_map = stencil(jnp.concatenate([empty, density, empty]), along_coeff, across_coeff)

    def pick(table, key, key_count):
        table_hi = lax.reduce_precision(table, exponent_bits=8, mantissa_bits=7)
        table_parts = jnp.concatenate(
            [table_hi.astype(jnp.bfloat16), (table - table_hi).astype(jnp.bfloat16)], axis=1
        ).T
        pick_row = (jnp.arange(key_count, dtype=jnp.int32)[:, None] == key[None, :]).astype(
            jnp.bfloat16
        )
        picked = jnp.dot(table_parts, pick_row, preferred_element_type=jnp.float32)
        picked = picked[:grid_y] + picked[grid_y:]
        return jnp.sum(jnp.where(pick_col, picked, 0.0), axis=0)

    pick_col = jnp.arange(grid_y, dtype=jnp.int32)[:, None] == got_y[None, :]
    force_here = pick(force_map.reshape(SL_DEV * grid_x, grid_y), row_key, SL_DEV * grid_x)
    below_density = halo_below[:grid_x]
    halo_force = jnp.concatenate([-along_coeff * below_density, along_coeff * above]).reshape(
        2 * grid_x, grid_y
    )
    halo_key = jnp.where(
        got_slice == 0, got_x, jnp.where(got_slice == SL_DEV - 1, got_x + grid_x, -1)
    )
    halo_here = pick(halo_force, halo_key, 2 * grid_x)
    kicked = got_energy + (force_here + halo_here)

    radiation = jnp.zeros((2, SL_DEV), jnp.float32)
    for period in range(PERIODS):
        if period == 0:
            cosine, sine_part = cosine0, sine0
            radiation = radiation + radiation0
        else:
            cosine, sine_part, local_sums = local_bunching(got_phase)
            cosine, sine_part = lax.optimization_barrier((cosine, sine_part))
            bunching = pb_sum_small(local_sums, "pb")
            radiation = radiation + couple * bunching
        real_here = jnp.sum(select * radiation[0][:, None], axis=0)
        imag_here = jnp.sum(select * radiation[1][:, None], axis=0)
        kicked = kicked + KICK_GAIN * profile * (real_here * cosine - imag_here * sine_part)
        got_phase = got_phase + SLIP_GAIN * kicked
        if period == 0:
            incoming = halo_below[grid_x, :2].reshape(2, 1)
        else:
            incoming = shifted(radiation[:, -1:], "ta", 1)
        radiation = jnp.concatenate([incoming, radiation[:, :-1]], axis=1)
    filled = arrived_weight > 0
    result = jnp.stack([jnp.where(filled, got_phase, 0.0), jnp.where(filled, kicked, 0.0)])
    return (result, radiation)


def solution(mesh):
    return jax.shard_map(
        body,
        mesh=mesh,
        in_specs=(
            P(None, ("ta", "pb")),
            P(("ta", "pb")),
            P(("ta", "pb")),
            P(("ta", "pb"), None),
            P(("ta", "pb")),
            P(),
            P(),
            P(),
            P(),
            P(),
            P(),
        ),
        out_specs=(P(None, ("ta", "pb")), P(None, "ta")),
        check_vma=False,
    )
```

```python
import math

import jax
import jax.numpy as jnp
from jax import lax
from jax.sharding import PartitionSpec as P

SL_DEV = 4
PS_DEV = 1024
HARM = 48
PERIODS = 2


DISPERSION = 3.0
LASER_GAIN = 1.0
KICK_GAIN = 0.5
SLIP_GAIN = 0.05


def shifted(value, axis, steps):
    count = lax.axis_size(axis)
    leading, last = (max(0, -steps), min(count, count - steps))
    return lax.ppermute(value, axis, [(source, source + steps) for source in range(leading, last)])


def lookup(values_table, positions):
    matches = positions[None, :] == jnp.arange(values_table.shape[0], dtype=jnp.int32)[:, None]
    return jnp.sum(jnp.where(matches, values_table[:, None], 0.0), axis=0)


def split3(x):
    hi = lax.reduce_precision(x, exponent_bits=8, mantissa_bits=7)
    rest = x - hi
    mid = lax.reduce_precision(rest, exponent_bits=8, mantissa_bits=7)
    lo = rest - mid
    return [part.astype(jnp.bfloat16) for part in (hi, mid, lo)]


def arrival_slots(to_group):
    groups, count = to_group.shape
    block_size = math.gcd(count, 512)
    turn_count = count // block_size
    onehot = to_group.astype(jnp.bfloat16).reshape(groups, turn_count, block_size)
    earlier = (jnp.arange(block_size)[:, None] > jnp.arange(block_size)[None, :]).astype(
        jnp.bfloat16
    )
    within = jnp.einsum("gtj,ij->gti", onehot, earlier, preferred_element_type=jnp.float32)
    rows_f = onehot.astype(jnp.float32)
    per_turn = jnp.sum(rows_f, axis=2)
    offsets = jnp.cumsum(per_turn, axis=1) - per_turn
    arrival = jnp.sum((within + offsets[:, :, None]) * rows_f, axis=0)
    return arrival.reshape(count).astype(jnp.int32)


def deposit_rows(weight_bf16, row_key, col, targets, grid_y):
    left = jnp.where(
        row_key[None, :] == targets[:, None], weight_bf16[None, :], jnp.zeros((), jnp.bfloat16)
    )
    right = (jnp.arange(grid_y, dtype=jnp.int32)[:, None] == col[None, :]).astype(jnp.bfloat16)
    return lax.dot_general(
        left, right, (((1,), (1,)), ((), ())), preferred_element_type=jnp.float32
    )


def pb_sum(rows, axis):
    count = lax.axis_size(axis)
    chunks = rows.reshape((count, -1) + rows.shape[1:])
    mine = jnp.sum(lax.all_to_all(chunks, axis, 0, 0, tiled=True), axis=0)
    every = lax.all_to_all(jnp.broadcast_to(mine[None], chunks.shape), axis, 0, 0, tiled=True)
    return every.reshape(rows.shape)


def pb_sum_small(value, axis):
    count = lax.axis_size(axis)
    spread = jnp.broadcast_to(value[None], (count,) + value.shape)
    return jnp.sum(lax.all_to_all(spread, axis, 0, 0, tiled=True), axis=0)


def stencil(extended, coeff_long, coeff_cross):
    centre = extended[1:-1]
    along_diff = extended[2:] - extended[:-2]
    padded_x = jnp.pad(centre, ((0, 0), (1, 1), (0, 0)))
    across = padded_x[:, 2:, :] + padded_x[:, :-2, :]
    padded_y = jnp.pad(centre, ((0, 0), (0, 0), (1, 1)))
    upper_y = padded_y[:, :, 2:]
    lower_y = padded_y[:, :, :-2]
    return coeff_long[None] * along_diff + coeff_cross[None] * (
        4.0 * centre - across - upper_y - lower_y
    )


def body(
    particles,
    weights,
    cell_index,
    target_group,
    target_slice,
    laser_x,
    laser_y,
    mode_x,
    mode_y,
    along_coeff,
    across_coeff,
):
    groups = lax.axis_size("ta")
    splits = lax.axis_size("pb")
    grid_x = laser_x.shape[0]
    grid_y = laser_y.shape[0]
    cell_count = grid_x * grid_y
    per_device = particles.shape[1]
    capacity = 2 * per_device // groups
    slot_count = groups * capacity
    row_x = cell_index // grid_y
    row_y = cell_index % grid_y
    energy = particles[1] + LASER_GAIN * lookup(laser_x, row_x) * lookup(laser_y, row_y) * jnp.sin(
        particles[0]
    )
    phases = particles[0] + DISPERSION * energy
    destination = target_group.reshape(1, per_device)
    to_group = lax.optimization_barrier(destination == jnp.arange(groups, dtype=jnp.int32)[:, None])
    arrival = arrival_slots(to_group)

    values = jnp.stack(
        [
            phases,
            energy,
            weights.astype(jnp.float32),
            (target_slice * cell_count + cell_index).astype(jnp.float32),
        ]
    )
    value_count = values.shape[0]
    parts = split3(values)
    left = jnp.concatenate(
        [
            jnp.where(to_group[None], part[:, None, :], jnp.zeros((), jnp.bfloat16)).reshape(
                value_count * groups, per_device
            )
            for part in parts
        ]
    )
    to_slot = (arrival[:, None] == jnp.arange(capacity, dtype=jnp.int32)[None, :]).astype(
        jnp.bfloat16
    )
    placed = jnp.dot(left, to_slot, preferred_element_type=jnp.float32)
    rows = value_count * groups
    send = (placed[:rows] + placed[rows : 2 * rows]) + placed[2 * rows :]
    got = lax.all_to_all(
        send.reshape(value_count, groups, capacity), "ta", split_axis=1, concat_axis=1, tiled=True
    ).reshape(value_count, slot_count)

    got_phase = got[0]
    got_energy = got[1]
    arrived_weight = got[2]
    combined = got[3].astype(jnp.int32)
    got_slice = combined // cell_count
    got_cell = combined % cell_count
    got_x = got_cell // grid_y
    got_y = got_cell % grid_y
    row_key = got_slice * grid_x + got_x
    weight_bf16 = arrived_weight.astype(jnp.bfloat16)

    density_rows = SL_DEV * grid_x
    partial = deposit_rows(
        weight_bf16, row_key, got_y, jnp.arange(density_rows, dtype=jnp.int32), grid_y
    )

    profile = lookup(mode_x, got_x) * lookup(mode_y, got_y)
    weighted = arrived_weight * profile
    select = (got_slice[None, :] == jnp.arange(SL_DEV, dtype=jnp.int32)[:, None]).astype(
        jnp.float32
    )

    def local_bunching(phase):
        harmonic_phase = HARM * phase
        cosine = jnp.cos(harmonic_phase)
        sine_part = jnp.sin(harmonic_phase)
        sums = jnp.stack(
            [
                jnp.sum(select * (weighted * cosine)[None, :], axis=1),
                jnp.sum(select * (-weighted * sine_part)[None, :], axis=1),
            ]
        )
        return cosine, sine_part, sums

    cosine0, sine0, sums0 = local_bunching(got_phase)
    lanes = -(-(grid_y + 2 * SL_DEV) // 128) * 128
    chunk_rows = -(-density_rows // (splits * 8)) * 8
    side = jnp.pad(
        sums0.reshape(1, 2 * SL_DEV),
        ((0, chunk_rows * splits - 1), (0, lanes - grid_y - 2 * SL_DEV)),
    )
    stacked = jnp.pad(partial, ((0, chunk_rows * splits - density_rows), (0, 0)))
    stacked = jnp.concatenate([stacked, side], axis=1)
    summed = pb_sum(stacked, "pb")
    density = summed[:density_rows, :grid_y].reshape(SL_DEV, grid_x, grid_y)
    bunching0 = summed[0, grid_y : grid_y + 2 * SL_DEV].reshape(2, SL_DEV)

    couple = 1.0 / math.sqrt(splits * PS_DEV)
    radiation0 = couple * bunching0
    last_row = jnp.pad(radiation0[:, -1:].reshape(1, 2), ((0, 7), (0, grid_y - 2)))
    halo_below = shifted(jnp.concatenate([density[SL_DEV - 1], last_row]), "ta", 1)
    above = shifted(density[0], "ta", -1)
    empty = jnp.zeros((1, grid_x, grid_y), jnp.float32)
    force_map = stencil(jnp.concatenate([empty, density, empty]), along_coeff, across_coeff)

    def pick(table, key, key_count):
        table_hi = lax.reduce_precision(table, exponent_bits=8, mantissa_bits=7)
        table_parts = jnp.concatenate(
            [table_hi.astype(jnp.bfloat16), (table - table_hi).astype(jnp.bfloat16)], axis=1
        ).T
        pick_row = (jnp.arange(key_count, dtype=jnp.int32)[:, None] == key[None, :]).astype(
            jnp.bfloat16
        )
        picked = jnp.dot(table_parts, pick_row, preferred_element_type=jnp.float32)
        picked = picked[:grid_y] + picked[grid_y:]
        return jnp.sum(jnp.where(pick_col, picked, 0.0), axis=0)

    pick_col = jnp.arange(grid_y, dtype=jnp.int32)[:, None] == got_y[None, :]
    force_here = pick(force_map.reshape(SL_DEV * grid_x, grid_y), row_key, SL_DEV * grid_x)
    below_density = halo_below[:grid_x]
    halo_force = jnp.concatenate([-along_coeff * below_density, along_coeff * above]).reshape(
        2 * grid_x, grid_y
    )
    halo_key = jnp.where(
        got_slice == 0, got_x, jnp.where(got_slice == SL_DEV - 1, got_x + grid_x, -1)
    )
    halo_here = pick(halo_force, halo_key, 2 * grid_x)
    kicked = got_energy + (force_here + halo_here)

    radiation = jnp.zeros((2, SL_DEV), jnp.float32)
    for period in range(PERIODS):
        if period == 0:
            cosine, sine_part = cosine0, sine0
            radiation = radiation + radiation0
        else:
            harmonic_phase = HARM * got_phase
            cosine = jnp.cos(harmonic_phase)
            sine_part = jnp.sin(harmonic_phase)
            cosine, sine_part = lax.optimization_barrier((cosine, sine_part))
            terms = jnp.stack([weighted * cosine, -weighted * sine_part])
            spread = jnp.einsum(
                "kcn,jn->kcj",
                jnp.broadcast_to(terms[None], (splits,) + terms.shape),
                select,
                precision=lax.Precision.HIGHEST,
            )
            bunching = jnp.sum(lax.all_to_all(spread, "pb", 0, 0, tiled=True), axis=0)
            radiation = radiation + couple * bunching
        real_here = jnp.sum(select * radiation[0][:, None], axis=0)
        imag_here = jnp.sum(select * radiation[1][:, None], axis=0)
        kicked = kicked + KICK_GAIN * profile * (real_here * cosine - imag_here * sine_part)
        got_phase = got_phase + SLIP_GAIN * kicked
        if period == 0:
            incoming = halo_below[grid_x, :2].reshape(2, 1)
        else:
            incoming = shifted(radiation[:, -1:], "ta", 1)
        radiation = jnp.concatenate([incoming, radiation[:, :-1]], axis=1)
    filled = arrived_weight > 0
    result = jnp.stack([jnp.where(filled, got_phase, 0.0), jnp.where(filled, kicked, 0.0)])
    return (result, radiation)


def solution(mesh):
    return jax.shard_map(
        body,
        mesh=mesh,
        in_specs=(
            P(None, ("ta", "pb")),
            P(("ta", "pb")),
            P(("ta", "pb")),
            P(("ta", "pb"), None),
            P(("ta", "pb")),
            P(),
            P(),
            P(),
            P(),
            P(),
            P(),
        ),
        out_specs=(P(None, ("ta", "pb")), P(None, "ta")),
        check_vma=False,
    )
```

```python
import math

import jax
import jax.numpy as jnp
from jax import lax
from jax.sharding import PartitionSpec as P

SL_DEV = 4
PS_DEV = 1024
HARM = 48
PERIODS = 2


DISPERSION = 3.0
LASER_GAIN = 1.0
KICK_GAIN = 0.5
SLIP_GAIN = 0.05


def shifted(value, axis, steps):
    count = lax.axis_size(axis)
    leading, last = (max(0, -steps), min(count, count - steps))
    return lax.ppermute(value, axis, [(source, source + steps) for source in range(leading, last)])


def lookup(values_table, positions):
    matches = positions[None, :] == jnp.arange(values_table.shape[0], dtype=jnp.int32)[:, None]
    return jnp.sum(jnp.where(matches, values_table[:, None], 0.0), axis=0)


def split3(x):
    hi = lax.reduce_precision(x, exponent_bits=8, mantissa_bits=7)
    rest = x - hi
    mid = lax.reduce_precision(rest, exponent_bits=8, mantissa_bits=7)
    lo = rest - mid
    return [part.astype(jnp.bfloat16) for part in (hi, mid, lo)]


def arrival_slots(to_group):
    groups, count = to_group.shape
    block_size = math.gcd(count, 512)
    turn_count = count // block_size
    onehot = to_group.astype(jnp.bfloat16).reshape(groups, turn_count, block_size)
    earlier = (jnp.arange(block_size)[:, None] > jnp.arange(block_size)[None, :]).astype(
        jnp.bfloat16
    )
    within = jnp.einsum("gtj,ij->gti", onehot, earlier, preferred_element_type=jnp.float32)
    rows_f = onehot.astype(jnp.float32)
    per_turn = jnp.sum(rows_f, axis=2)
    offsets = jnp.cumsum(per_turn, axis=1) - per_turn
    arrival = jnp.sum((within + offsets[:, :, None]) * rows_f, axis=0)
    return arrival.reshape(count).astype(jnp.int32)


def deposit_rows(weight_bf16, row_key, col, targets, grid_y):
    left = jnp.where(
        row_key[None, :] == targets[:, None], weight_bf16[None, :], jnp.zeros((), jnp.bfloat16)
    )
    right = (jnp.arange(grid_y, dtype=jnp.int32)[:, None] == col[None, :]).astype(jnp.bfloat16)
    return lax.dot_general(
        left, right, (((1,), (1,)), ((), ())), preferred_element_type=jnp.float32
    )


def pb_sum(rows, axis):
    count = lax.axis_size(axis)
    chunks = rows.reshape((count, -1) + rows.shape[1:])
    mine = jnp.sum(lax.all_to_all(chunks, axis, 0, 0, tiled=True), axis=0)
    every = lax.all_to_all(jnp.broadcast_to(mine[None], chunks.shape), axis, 0, 0, tiled=True)
    return every.reshape(rows.shape)


def pb_sum_small(value, axis):
    count = lax.axis_size(axis)
    spread = jnp.broadcast_to(value[None], (count,) + value.shape)
    return jnp.sum(lax.all_to_all(spread, axis, 0, 0, tiled=True), axis=0)


def stencil(extended, coeff_long, coeff_cross):
    centre = extended[1:-1]
    along_diff = extended[2:] - extended[:-2]
    padded_x = jnp.pad(centre, ((0, 0), (1, 1), (0, 0)))
    across = padded_x[:, 2:, :] + padded_x[:, :-2, :]
    padded_y = jnp.pad(centre, ((0, 0), (0, 0), (1, 1)))
    upper_y = padded_y[:, :, 2:]
    lower_y = padded_y[:, :, :-2]
    return coeff_long[None] * along_diff + coeff_cross[None] * (
        4.0 * centre - across - upper_y - lower_y
    )


def body(
    particles,
    weights,
    cell_index,
    target_group,
    target_slice,
    laser_x,
    laser_y,
    mode_x,
    mode_y,
    along_coeff,
    across_coeff,
):
    groups = lax.axis_size("ta")
    splits = lax.axis_size("pb")
    grid_x = laser_x.shape[0]
    grid_y = laser_y.shape[0]
    cell_count = grid_x * grid_y
    per_device = particles.shape[1]
    capacity = 2 * per_device // groups
    slot_count = groups * capacity
    row_x = cell_index // grid_y
    row_y = cell_index % grid_y
    energy = particles[1] + LASER_GAIN * lookup(laser_x, row_x) * lookup(laser_y, row_y) * jnp.sin(
        particles[0]
    )
    phases = particles[0] + DISPERSION * energy
    destination = target_group.reshape(1, per_device)
    to_group = lax.optimization_barrier(destination == jnp.arange(groups, dtype=jnp.int32)[:, None])
    arrival = arrival_slots(to_group)

    values = jnp.stack(
        [
            phases,
            energy,
            weights.astype(jnp.float32),
            (target_slice * cell_count + cell_index).astype(jnp.float32),
        ]
    )
    value_count = values.shape[0]
    parts = split3(values)
    left = jnp.concatenate(
        [
            jnp.where(to_group[None], part[:, None, :], jnp.zeros((), jnp.bfloat16)).reshape(
                value_count * groups, per_device
            )
            for part in parts
        ]
    )
    to_slot = (arrival[:, None] == jnp.arange(capacity, dtype=jnp.int32)[None, :]).astype(
        jnp.bfloat16
    )
    placed = jnp.dot(left, to_slot, preferred_element_type=jnp.float32)
    rows = value_count * groups
    send = (placed[:rows] + placed[rows : 2 * rows]) + placed[2 * rows :]
    got = lax.all_to_all(
        send.reshape(value_count, groups, capacity), "ta", split_axis=1, concat_axis=1, tiled=True
    ).reshape(value_count, slot_count)

    got_phase = got[0]
    got_energy = got[1]
    arrived_weight = got[2]
    combined = got[3].astype(jnp.int32)
    got_slice = combined // cell_count
    got_cell = combined % cell_count
    got_x = got_cell // grid_y
    got_y = got_cell % grid_y
    row_key = got_slice * grid_x + got_x
    weight_bf16 = arrived_weight.astype(jnp.bfloat16)

    density_rows = SL_DEV * grid_x
    partial = deposit_rows(
        weight_bf16, row_key, got_y, jnp.arange(density_rows, dtype=jnp.int32), grid_y
    )

    profile = lookup(mode_x, got_x) * lookup(mode_y, got_y)
    weighted = arrived_weight * profile
    select = (got_slice[None, :] == jnp.arange(SL_DEV, dtype=jnp.int32)[:, None]).astype(
        jnp.float32
    )

    def local_bunching(phase):
        harmonic_phase = HARM * phase
        cosine = jnp.cos(harmonic_phase)
        sine_part = jnp.sin(harmonic_phase)
        sums = jnp.stack(
            [
                jnp.sum(select * (weighted * cosine)[None, :], axis=1),
                jnp.sum(select * (-weighted * sine_part)[None, :], axis=1),
            ]
        )
        return cosine, sine_part, sums

    cosine0, sine0, sums0 = local_bunching(got_phase)
    lanes = -(-(grid_y + 2 * SL_DEV) // 128) * 128
    chunk_rows = -(-density_rows // (splits * 8)) * 8
    side = jnp.pad(
        sums0.reshape(1, 2 * SL_DEV),
        ((0, chunk_rows * splits - 1), (0, lanes - grid_y - 2 * SL_DEV)),
    )
    stacked = jnp.pad(partial, ((0, chunk_rows * splits - density_rows), (0, 0)))
    stacked = jnp.concatenate([stacked, side], axis=1)
    summed = pb_sum(stacked, "pb")
    density = summed[:density_rows, :grid_y].reshape(SL_DEV, grid_x, grid_y)
    bunching0 = summed[0, grid_y : grid_y + 2 * SL_DEV].reshape(2, SL_DEV)

    couple = 1.0 / math.sqrt(splits * PS_DEV)
    radiation0 = couple * bunching0
    last_lanes = jnp.pad(radiation0[:, -1:].reshape(1, 2), ((0, grid_x - 1), (0, lanes - grid_y - 2)))
    halo_below = shifted(jnp.concatenate([density[SL_DEV - 1], last_lanes], axis=1), "ta", 1)
    above = shifted(jnp.pad(density[0], ((0, 0), (0, lanes - grid_y))), "ta", -1)[:, :grid_y]
    empty = jnp.zeros((1, grid_x, grid_y), jnp.float32)
    force_map = stencil(jnp.concatenate([empty, density, empty]), along_coeff, across_coeff)

    def pick(table, key, key_count):
        table_hi = lax.reduce_precision(table, exponent_bits=8, mantissa_bits=7)
        table_parts = jnp.concatenate(
            [table_hi.astype(jnp.bfloat16), (table - table_hi).astype(jnp.bfloat16)], axis=1
        ).T
        pick_row = (jnp.arange(key_count, dtype=jnp.int32)[:, None] == key[None, :]).astype(
            jnp.bfloat16
        )
        picked = jnp.dot(table_parts, pick_row, preferred_element_type=jnp.float32)
        picked = picked[:grid_y] + picked[grid_y:]
        return jnp.sum(jnp.where(pick_col, picked, 0.0), axis=0)

    pick_col = jnp.arange(grid_y, dtype=jnp.int32)[:, None] == got_y[None, :]
    force_here = pick(force_map.reshape(SL_DEV * grid_x, grid_y), row_key, SL_DEV * grid_x)
    below_density = halo_below[:, :grid_y]
    halo_force = jnp.concatenate([-along_coeff * below_density, along_coeff * above]).reshape(
        2 * grid_x, grid_y
    )
    halo_key = jnp.where(
        got_slice == 0, got_x, jnp.where(got_slice == SL_DEV - 1, got_x + grid_x, -1)
    )
    halo_here = pick(halo_force, halo_key, 2 * grid_x)
    kicked = got_energy + (force_here + halo_here)

    radiation = jnp.zeros((2, SL_DEV), jnp.float32)
    for period in range(PERIODS):
        if period == 0:
            cosine, sine_part = cosine0, sine0
            radiation = radiation + radiation0
        else:
            cosine, sine_part, local_sums = local_bunching(got_phase)
            cosine, sine_part = lax.optimization_barrier((cosine, sine_part))
            bunching = pb_sum_small(local_sums, "pb")
            radiation = radiation + couple * bunching
        real_here = jnp.sum(select * radiation[0][:, None], axis=0)
        imag_here = jnp.sum(select * radiation[1][:, None], axis=0)
        kicked = kicked + KICK_GAIN * profile * (real_here * cosine - imag_here * sine_part)
        got_phase = got_phase + SLIP_GAIN * kicked
        if period == 0:
            incoming = halo_below[0, grid_y : grid_y + 2].reshape(2, 1)
        else:
            incoming = shifted(radiation[:, -1:], "ta", 1)
        radiation = jnp.concatenate([incoming, radiation[:, :-1]], axis=1)
    filled = arrived_weight > 0
    result = jnp.stack([jnp.where(filled, got_phase, 0.0), jnp.where(filled, kicked, 0.0)])
    return (result, radiation)


def solution(mesh):
    return jax.shard_map(
        body,
        mesh=mesh,
        in_specs=(
            P(None, ("ta", "pb")),
            P(("ta", "pb")),
            P(("ta", "pb")),
            P(("ta", "pb"), None),
            P(("ta", "pb")),
            P(),
            P(),
            P(),
            P(),
            P(),
            P(),
        ),
        out_specs=(P(None, ("ta", "pb")), P(None, "ta")),
        check_vma=False,
    )
```
